32 devices in a mesh: ctx: 8 (over z, y), seq: 4 (over x, core).
Axes of the slice: x: 2, y: 2, z: 4, core: 2. Of those that a mesh axis runs over, the one named last changes fastest.
Arguments:
- queries: bfloat16 [32768, 2048], P(('ctx', 'seq')), may hold values from -6 to 6
- keys: bfloat16 [32768, 2048], P(('ctx', 'seq')), may hold values from -6 to 6
- values: bfloat16 [32768, 2048], P(('ctx', 'seq')), may hold values from -6 to 6
- mixing: float32 [10, 16, 32768], P(None, None, ('ctx', 'seq')), may hold values from 0 to 1, as said below
Outputs:
- attended: float32 [32768, 2048], P(('ctx', 'seq'))
The draws below stay inside these ranges and needn't reach their ends.
Inputs may be any that keep to these rules, and one draw needn't show every extreme that they name: Every mixing weight is positive and at most 1.
All inputs are finite; a program needn't handle non-finite values.
Results may differ from the reference program's by a relative error of at most 0.0028.
Values sent between devices are 32-bit elements; how exact they have to be, the bound alone decides.
No kernel may reach another device: no remote copies, remote signals or barrier semaphores. Data moves between devices by JAX's collectives and lax.ppermute only.
A program may use at most 192 MiB of HBM per device.

```python
import math
import jax
import jax.numpy as jnp
from jax import lax

H = 16
DK = 128
DV = 128
SPAN = 64
TOK_DEV = 1024
LOCAL_BITS = 4
DEV_BITS = 5
TREE_LEVELS = 10
TOKENS = 32768
N_CTX = 8
N_SEQ = 4


def draw_mixing(key, part):
    level_axis = jnp.arange(TREE_LEVELS, dtype=jnp.float32)[:, None, None]
    base_scale = jnp.power(SPAN * jnp.power(2.0, level_axis), -0.5)
    level_factor = jnp.exp(jax.random.uniform(key, (TREE_LEVELS, H, TOKENS), jnp.float32, math.log(0.25), math.log(2.0)))
    return (level_factor * base_scale).astype(jnp.float32)


def block_levels(key, shape, shards, low, high):
    factor_of, own = 1.0, jax.random.fold_in(key, 6)
    for dim, shards_of in shards:
        steps = jnp.exp(jax.random.uniform(jax.random.fold_in(own, dim), (shards_of,), jnp.float32, low / len(shards), high / len(shards)))
        factor_of = factor_of * jnp.repeat(steps, shape[dim] // shards_of).reshape([-1 if axis == dim else 1 for axis in range(len(shape))])
    return factor_of


def noise(own_key, dims, deviation, bound, split=(), kind=jnp.bfloat16):
    drawn = deviation * jax.random.normal(own_key, dims, jnp.float32)
    if split:
        drawn = drawn * block_levels(own_key, dims, split, -0.22, 0.18)
    return jnp.clip(drawn, -bound, bound).astype(kind)


def setup_inputs(seed: int = 0) -> dict:
    streams_of = jax.random.split(jax.random.key(seed), 5)
    return {
        "queries": noise(streams_of[0], (TOKENS, H * DK), 1.0, 6.0, ((0, 32),)),
        "keys": noise(streams_of[1], (TOKENS, H * DK), 1.0, 6.0, ((0, 32),)),
        "values": noise(streams_of[2], (TOKENS, H * DV), 1.0, 6.0, ((0, 32),)),
        "mixing": draw_mixing(jax.random.fold_in(streams_of[4], 71), 0),
    }


def weighted_local(queries, keys, values, mixing, level_count):
    row_count = queries.shape[0]
    head_count = mixing.shape[1]
    key_width = queries.shape[1] // head_count
    value_width = values.shape[1] // head_count
    scale_factor = key_width ** -0.5
    positions = jnp.arange(row_count, dtype=jnp.int32)
    span_of = positions // SPAN
    crossed = jnp.bitwise_xor(span_of[:, None], span_of[None, :])
    level_map = jnp.zeros((row_count, row_count), jnp.int32)
    for power_index in range(level_count - 1):
        level_map = level_map + (crossed >= 2 ** power_index).astype(jnp.int32)
    causal = positions[:, None] >= positions[None, :]

    def one_head(head_index):
        query_head = lax.dynamic_slice_in_dim(queries, head_index * key_width, key_width, 1)
        key_head = lax.dynamic_slice_in_dim(keys, head_index * key_width, key_width, 1)
        value_head = lax.dynamic_slice_in_dim(values, head_index * value_width, value_width, 1)
        scores = jnp.dot(query_head, key_head.T, preferred_element_type=jnp.float32) * scale_factor
        head_mix = lax.dynamic_index_in_dim(mixing, head_index, 1, keepdims=False)
        weights = jnp.zeros_like(scores)
        for level_index in range(level_count):
            weights = weights + jnp.where(level_map == level_index, head_mix[level_index][:, None], 0.0)
        mixed_scores = jnp.where(causal, scores * weights, 0.0).astype(jnp.bfloat16)
        return jnp.dot(mixed_scores, value_head, preferred_element_type=jnp.float32)

    per_head = lax.map(one_head, jnp.arange(head_count, dtype=jnp.int32))
    return per_head.transpose(1, 0, 2).reshape(row_count, head_count * value_width)


def reference(queries, keys, values, mixing):
    devices_all = N_CTX * N_SEQ
    level_count = LOCAL_BITS + 1
    scale_factor = DK ** -0.5
    query_blocks = queries.reshape(devices_all, TOK_DEV, H * DK)
    key_blocks = keys.reshape(devices_all, TOK_DEV, H * DK)
    value_blocks = values.reshape(devices_all, TOK_DEV, H * DV)
    mix_blocks = mixing.reshape(TREE_LEVELS, H, devices_all, TOK_DEV).transpose(2, 0, 1, 3)

    def state_of(pair):
        key_portion = pair[0].reshape(TOK_DEV, H, DK).astype(jnp.float32)
        value_portion = pair[1].reshape(TOK_DEV, H, DV).astype(jnp.float32)
        return jnp.einsum("xej,xec->ejc", key_portion, value_portion)

    states = lax.map(state_of, (key_blocks, value_blocks))
    block_list = []
    for bit_index in range(DEV_BITS):
        grouped = states.reshape(devices_all >> (bit_index + 1), 2, 2 ** bit_index, H, DK, DV)
        block_list.append(jnp.sum(grouped[:, 0], axis=1).astype(jnp.bfloat16))

    def one_device(index):
        local_out = weighted_local(query_blocks[index], key_blocks[index], value_blocks[index], mix_blocks[index], level_count)
        query_head_rows = query_blocks[index].reshape(TOK_DEV, H, DK).astype(jnp.float32)
        cross = jnp.zeros((TOK_DEV, H, DV), jnp.float32)
        for bit_index in range(DEV_BITS):
            sibling_node = block_list[bit_index][index >> (bit_index + 1)].astype(jnp.float32)
            flag = ((index >> bit_index) & 1).astype(jnp.float32)
            level_mix = mix_blocks[index][level_count + bit_index].T
            weight_now = flag * level_mix * scale_factor
            level_term = jnp.einsum("cxm,xms->cxs", query_head_rows, sibling_node)
            cross = cross + weight_now[:, :, None] * level_term
        return local_out + cross.reshape(TOK_DEV, H * DV)

    outputs = lax.map(one_device, jnp.arange(devices_all, dtype=jnp.int32))
    return outputs.reshape(TOKENS, H * DV)
```

```python
import functools

import numpy as np
import jax
import jax.numpy as jnp
from jax import lax
from jax.experimental import pallas as pl
from jax.experimental.pallas import tpu as pltpu
from jax.sharding import PartitionSpec as P

SPAN = 64
TQ = 256
CHUNKS = 4


def level_masks(block, level_count):
    pos = np.arange(block)
    span = pos // SPAN
    crossed = span[:, None] ^ span[None, :]
    level = np.zeros_like(crossed)
    for power_index in range(level_count - 1):
        level = level + (crossed >= 2**power_index)
    causal = pos[:, None] >= pos[None, :]
    inner = int(np.log2(block // SPAN)) + 1
    return np.stack(
        [((level == l) & causal).astype(np.float32) for l in range(inner)]
    )


def state_kernel(k_ref, v_ref, o_ref):
    o_ref[0] = lax.dot_general(
        k_ref[...], v_ref[...], (((0,), (0,)), ((), ())),
        preferred_element_type=jnp.float32,
    )


def own_state(keys, values, head_count):
    rows, width = keys.shape
    dk = width // head_count
    dv = values.shape[1] // head_count
    return pl.pallas_call(
        state_kernel,
        grid=(head_count,),
        in_specs=[
            pl.BlockSpec((rows, dk), lambda h: (0, h)),
            pl.BlockSpec((rows, dv), lambda h: (0, h)),
        ],
        out_specs=pl.BlockSpec((1, dk, dv), lambda h: (h, 0, 0)),
        out_shape=jax.ShapeDtypeStruct((head_count, dk, dv), jnp.float32),
        cost_estimate=pl.CostEstimate(
            flops=2 * rows * dk * dv * head_count,
            bytes_accessed=2 * rows * (dk + dv) * head_count + 4 * dk * dv * head_count,
            transcendentals=0,
        ),
    )(keys, values)


def local_kernel(scale, rows, q_ref, k_ref, v_ref, m_ref, c_ref, o_ref):
    blocks = rows // TQ
    inner = c_ref.shape[0]
    for a in range(blocks):
        r0 = a * TQ
        qb = q_ref[r0:r0 + TQ, :]
        kk = k_ref[0:r0 + TQ, :]
        s = lax.dot_general(
            qb, kk, (((1,), (1,)), ((), ())), preferred_element_type=jnp.float32
        )
        s = s * scale
        mix = m_ref[0, r0:r0 + TQ, :]
        pieces = []
        for b in range(a):
            level = inner + (a ^ b).bit_length() - 1
            w = mix[:, level:level + 1]
            pieces.append((s[:, b * TQ:(b + 1) * TQ] * w).astype(jnp.bfloat16))
        wd = c_ref[0] * mix[:, 0:1]
        for l in range(1, inner):
            wd = wd + c_ref[l] * mix[:, l:l + 1]
        pieces.append((s[:, r0:r0 + TQ] * wd).astype(jnp.bfloat16))
        p = pieces[0] if len(pieces) == 1 else jnp.concatenate(pieces, axis=1)
        o_ref[r0:r0 + TQ, :] = jnp.dot(
            p, v_ref[0:r0 + TQ, :], preferred_element_type=jnp.float32
        )


def local_part(queries, keys, values, mix_t, masks, first, count, scale):
    rows = queries.shape[0]
    head_count = mix_t.shape[0]
    dk = queries.shape[1] // head_count
    dv = values.shape[1] // head_count
    levels = mix_t.shape[2]
    blocks = rows // TQ
    tiles = blocks * (blocks + 1) // 2
    return pl.pallas_call(
        functools.partial(local_kernel, scale, rows),
        grid=(count,),
        in_specs=[
            pl.BlockSpec((rows, dk), lambda h: (0, h + first)),
            pl.BlockSpec((rows, dk), lambda h: (0, h + first)),
            pl.BlockSpec((rows, dv), lambda h: (0, h + first)),
            pl.BlockSpec((1, rows, levels), lambda h: (h + first, 0, 0)),
            pl.BlockSpec(masks.shape, lambda h: (0, 0, 0)),
        ],
        out_specs=pl.BlockSpec((rows, dv), lambda h: (0, h)),
        out_shape=jax.ShapeDtypeStruct((rows, dv * count), jnp.float32),
        cost_estimate=pl.CostEstimate(
            flops=2 * tiles * TQ * TQ * (dk + dv) * count,
            bytes_accessed=(2 * rows * (2 * dk + dv) + 4 * rows * dv) * count,
            transcendentals=0,
        ),
        compiler_params=pltpu.CompilerParams(vmem_limit_bytes=64 * 1024 * 1024),
    )(queries, keys, values, mix_t, masks)


def cross_kernel(scale, rows, first_level, q_ref, s_ref, m_ref, l_ref, *rest):
    o_ref = rest[-1]
    bits = s_ref.shape[0]
    sib = jnp.concatenate([s_ref[b, 0] for b in range(bits)], axis=1)
    dv = s_ref.shape[3]
    for a in range(rows // TQ):
        r0 = a * TQ
        t = jnp.dot(q_ref[r0:r0 + TQ, :], sib, preferred_element_type=jnp.float32)
        mix = m_ref[0, r0:r0 + TQ, :]
        cross = jnp.zeros((TQ, dv), jnp.float32)
        for b in range(bits):
            w = mix[:, first_level + b:first_level + b + 1] * scale
            cross = cross + w * t[:, b * dv:(b + 1) * dv]
        o_ref[r0:r0 + TQ, :] = l_ref[r0:r0 + TQ, :] + cross


def cross_part(queries, sibs, mix_t, local, first, count, scale, first_level, prev):
    rows = queries.shape[0]
    head_count = mix_t.shape[0]
    dk = queries.shape[1] // head_count
    dv = sibs.shape[3]
    levels = mix_t.shape[2]
    bits = sibs.shape[0]
    in_specs = [
        pl.BlockSpec((rows, dk), lambda h: (0, h + first)),
        pl.BlockSpec((bits, 1, dk, dv), lambda h: (0, h + first, 0, 0)),
        pl.BlockSpec((1, rows, levels), lambda h: (h + first, 0, 0)),
        pl.BlockSpec((rows, dv), lambda h: (0, h)),
    ]
    operands = [queries, sibs, mix_t, local]
    aliases = {}
    if prev is not None:
        in_specs.append(pl.BlockSpec(memory_space=pl.ANY))
        operands.append(prev)
        aliases = {4: 0}
    return pl.pallas_call(
        functools.partial(cross_kernel, scale, rows, first_level),
        grid=(count,),
        in_specs=in_specs,
        out_specs=pl.BlockSpec((rows, dv), lambda h: (0, h + first)),
        out_shape=jax.ShapeDtypeStruct((rows, dv * head_count), jnp.float32),
        input_output_aliases=aliases,
        cost_estimate=pl.CostEstimate(
            flops=2 * rows * dk * dv * bits * count,
            bytes_accessed=(2 * rows * dk + 8 * rows * dv) * count,
            transcendentals=0,
        ),
        compiler_params=pltpu.CompilerParams(vmem_limit_bytes=64 * 1024 * 1024),
    )(*operands)


def swap(block, axis, bit, one_way=False):
    count = lax.axis_size(axis)
    route = []
    for low in range(count):
        high = low | 1 << bit
        if high != low and high < count:
            route.append((low, high))
            if not one_way:
                route.append((high, low))
    return lax.ppermute(block, axis, route)


def to_offset(block, axis, offset):
    count = lax.axis_size(axis)
    return lax.ppermute(block, axis, [(s, s ^ offset) for s in range(count)])


def shards(queries, keys, values, mixing):
    rows = queries.shape[0]
    head_count = mixing.shape[1]
    dk = queries.shape[1] // head_count
    scale = dk ** (-0.5)
    level_count = (rows // SPAN).bit_length()
    mix_t = mixing.transpose(1, 2, 0)
    masks = jnp.asarray(level_masks(TQ, level_count))

    state = own_state(keys, values, head_count)

    seq_count = lax.axis_size("seq")
    ctx_count = lax.axis_size("ctx")
    seq_bits = seq_count.bit_length() - 1
    ctx_bits = ctx_count.bit_length() - 1
    seq_place = lax.axis_index("seq")
    ctx_place = lax.axis_index("ctx")

    sibs = []
    flags = []
    running = state
    half = head_count // 2
    for bit in range(seq_bits):
        if bit == 0 or seq_count < 4:
            partner = swap(running, "seq", bit)
        else:
            mine = seq_place & 1
            sent = lax.dynamic_slice_in_dim(running, mine * half, half, 0)
            got = swap(sent, "seq", bit)
            other = swap(got, "seq", 0)
            lo = jnp.where(mine == 0, got, other)
            hi = jnp.where(mine == 0, other, got)
            partner = jnp.concatenate([lo, hi], axis=0)
        sibs.append(partner)
        flags.append(seq_place >> bit & 1)
        running = running + partner

    share = head_count // seq_count
    quarter = lax.dynamic_slice_in_dim(running, seq_place * share, share, 0)
    ctx_sibs = []
    for bit in range(ctx_bits):
        got = swap(quarter, "ctx", bit, one_way=(bit == ctx_bits - 1))
        ctx_sibs.append(got)
        if bit != ctx_bits - 1:
            quarter = quarter + got

    for bit in range(ctx_bits):
        part = ctx_sibs[bit]
        parts = {0: part}
        for offset in range(1, seq_count):
            if offset & 1 and offset > 1:
                parts[offset] = to_offset(parts[offset ^ 1], "seq", 1)
            else:
                parts[offset] = to_offset(part, "seq", offset)
        full = []
        for owner in range(seq_count):
            pick = jnp.zeros_like(part)
            for offset in range(seq_count):
                pick = jnp.where((seq_place ^ offset) == owner, parts[offset], pick)
            full.append(pick)
        sibs.append(jnp.concatenate(full, axis=0))
        flags.append(ctx_place >> bit & 1)

    rounded = jnp.stack(
        [(flags[i].astype(jnp.float32) * sibs[i]).astype(jnp.bfloat16) for i in range(len(sibs))]
    )

    per = head_count // CHUNKS
    out = None
    for c in range(CHUNKS):
        local = local_part(queries, keys, values, mix_t, masks, c * per, per, scale)
        out = cross_part(queries, rounded, mix_t, local, c * per, per, scale, level_count, out)
    return out


def solution(mesh):
    return jax.shard_map(
        shards,
        mesh=mesh,
        in_specs=(
            P(("ctx", "seq"), None),
            P(("ctx", "seq"), None),
            P(("ctx", "seq"), None),
            P(None, None, ("ctx", "seq")),
        ),
        out_specs=P(("ctx", "seq"), None),
        check_vma=False,
    )
```

```python
import functools

import numpy as np
import jax
import jax.numpy as jnp
from jax import lax
from jax.experimental import pallas as pl
from jax.experimental.pallas import tpu as pltpu
from jax.sharding import PartitionSpec as P

SPAN = 64
TQ = 256
CHUNKS = 4
LOCAL_GROUP = 2
CROSS_GROUP = 4


def level_masks(block, level_count):
    pos = np.arange(block)
    span = pos // SPAN
    crossed = span[:, None] ^ span[None, :]
    level = np.zeros_like(crossed)
    for power_index in range(level_count - 1):
        level = level + (crossed >= 2**power_index)
    causal = pos[:, None] >= pos[None, :]
    inner = int(np.log2(block // SPAN)) + 1
    return np.stack(
        [((level == l) & causal).astype(np.float32) for l in range(inner)]
    )


def state_kernel(head_count, k_ref, v_ref, o_ref):
    @pl.when(pl.program_id(0) == 0)
    def _():
        o_ref[...] = jnp.zeros_like(o_ref)

    dk = o_ref.shape[1]
    dv = o_ref.shape[2]
    for h in range(head_count):
        o_ref[h] += lax.dot_general(
            k_ref[:, h * dk:(h + 1) * dk], v_ref[:, h * dv:(h + 1) * dv],
            (((0,), (0,)), ((), ())), preferred_element_type=jnp.float32,
        )


def own_state(keys, values, head_count):
    rows, width = keys.shape
    dk = width // head_count
    dv = values.shape[1] // head_count
    tr = min(rows, 512)
    return pl.pallas_call(
        functools.partial(state_kernel, head_count),
        grid=(rows // tr,),
        in_specs=[
            pl.BlockSpec((tr, width), lambda r: (r, 0)),
            pl.BlockSpec((tr, values.shape[1]), lambda r: (r, 0)),
        ],
        out_specs=pl.BlockSpec((head_count, dk, dv), lambda r: (0, 0, 0)),
        out_shape=jax.ShapeDtypeStruct((head_count, dk, dv), jnp.float32),
        cost_estimate=pl.CostEstimate(
            flops=2 * rows * dk * dv * head_count,
            bytes_accessed=2 * rows * (dk + dv) * head_count + 4 * dk * dv * head_count,
            transcendentals=0,
        ),
        compiler_params=pltpu.CompilerParams(vmem_limit_bytes=64 * 1024 * 1024),
    )(keys, values)


def local_kernel(scale, rows, group, q_ref, k_ref, v_ref, m_ref, c_ref, *rest):
    o_ref = rest[-1]
    blocks = rows // TQ
    inner = c_ref.shape[0]
    dk = q_ref.shape[1] // group
    dv = v_ref.shape[1] // group
    for j in range(group):
        qc = slice(j * dk, (j + 1) * dk)
        vc = slice(j * dv, (j + 1) * dv)
        for a in range(blocks):
            r0 = a * TQ
            s = lax.dot_general(
                q_ref[r0:r0 + TQ, qc], k_ref[0:r0 + TQ, qc],
                (((1,), (1,)), ((), ())), preferred_element_type=jnp.float32,
            )
            s = s * scale
            mix = m_ref[j, r0:r0 + TQ, :]
            pieces = []
            for b in range(a):
                level = inner + (a ^ b).bit_length() - 1
                w = mix[:, level:level + 1]
                pieces.append((s[:, b * TQ:(b + 1) * TQ] * w).astype(jnp.bfloat16))
            wd = c_ref[0] * mix[:, 0:1]
            for l in range(1, inner):
                wd = wd + c_ref[l] * mix[:, l:l + 1]
            pieces.append((s[:, r0:r0 + TQ] * wd).astype(jnp.bfloat16))
            p = pieces[0] if len(pieces) == 1 else jnp.concatenate(pieces, axis=1)
            o_ref[r0:r0 + TQ, vc] = jnp.dot(
                p, v_ref[0:r0 + TQ, vc], preferred_element_type=jnp.float32
            )


def local_part(queries, keys, values, mix_t, masks, first, count, group, scale, prev):
    rows = queries.shape[0]
    head_count = mix_t.shape[0]
    dk = queries.shape[1] // head_count
    dv = values.shape[1] // head_count
    levels = mix_t.shape[2]
    blocks = rows // TQ
    tiles = blocks * (blocks + 1) // 2
    base = first // group
    in_specs = [
        pl.BlockSpec((rows, dk * group), lambda h: (0, h + base)),
        pl.BlockSpec((rows, dk * group), lambda h: (0, h + base)),
        pl.BlockSpec((rows, dv * group), lambda h: (0, h + base)),
        pl.BlockSpec((group, rows, levels), lambda h: (h + base, 0, 0)),
        pl.BlockSpec(masks.shape, lambda h: (0, 0, 0)),
    ]
    operands = [queries, keys, values, mix_t, masks]
    aliases = {}
    if prev is not None:
        in_specs.append(pl.BlockSpec(memory_space=pl.ANY))
        operands.append(prev)
        aliases = {5: 0}
    return pl.pallas_call(
        functools.partial(local_kernel, scale, rows, group),
        grid=(count // group,),
        in_specs=in_specs,
        out_specs=pl.BlockSpec((rows, dv * group), lambda h: (0, h + base)),
        out_shape=jax.ShapeDtypeStruct((rows, dv * head_count), jnp.float32),
        input_output_aliases=aliases,
        cost_estimate=pl.CostEstimate(
            flops=2 * tiles * TQ * TQ * (dk + dv) * count,
            bytes_accessed=(2 * rows * (2 * dk + dv) + 4 * rows * dv) * count,
            transcendentals=0,
        ),
        compiler_params=pltpu.CompilerParams(vmem_limit_bytes=64 * 1024 * 1024),
    )(*operands)


def cross_kernel(scale, rows, first_level, group, q_ref, s_ref, m_ref, l_ref, o_ref):
    bits = s_ref.shape[0]
    dk = s_ref.shape[2]
    dv = s_ref.shape[3]
    for j in range(group):
        sib = jnp.concatenate([s_ref[b, j] for b in range(bits)], axis=1)
        for a in range(rows // TQ):
            r0 = a * TQ
            t = jnp.dot(
                q_ref[r0:r0 + TQ, j * dk:(j + 1) * dk], sib,
                preferred_element_type=jnp.float32,
            )
            mix = m_ref[j, r0:r0 + TQ, :]
            cross = jnp.zeros((TQ, dv), jnp.float32)
            for b in range(bits):
                w = mix[:, first_level + b:first_level + b + 1] * scale
                cross = cross + w * t[:, b * dv:(b + 1) * dv]
            o_ref[r0:r0 + TQ, j * dv:(j + 1) * dv] = (
                l_ref[r0:r0 + TQ, j * dv:(j + 1) * dv] + cross
            )


def cross_all(queries, sibs, mix_t, local, scale, first_level, group):
    rows = queries.shape[0]
    head_count = mix_t.shape[0]
    dk = queries.shape[1] // head_count
    dv = sibs.shape[3]
    levels = mix_t.shape[2]
    bits = sibs.shape[0]
    return pl.pallas_call(
        functools.partial(cross_kernel, scale, rows, first_level, group),
        grid=(head_count // group,),
        in_specs=[
            pl.BlockSpec((rows, dk * group), lambda g: (0, g)),
            pl.BlockSpec((bits, group, dk, dv), lambda g: (0, g, 0, 0)),
            pl.BlockSpec((group, rows, levels), lambda g: (g, 0, 0)),
            pl.BlockSpec((rows, dv * group), lambda g: (0, g)),
        ],
        out_specs=pl.BlockSpec((rows, dv * group), lambda g: (0, g)),
        out_shape=jax.ShapeDtypeStruct((rows, dv * head_count), jnp.float32),
        input_output_aliases={3: 0},
        cost_estimate=pl.CostEstimate(
            flops=2 * rows * dk * dv * bits * head_count,
            bytes_accessed=(2 * rows * dk + 8 * rows * dv) * head_count,
            transcendentals=0,
        ),
        compiler_params=pltpu.CompilerParams(vmem_limit_bytes=64 * 1024 * 1024),
    )(queries, sibs, mix_t, local)


def swap(block, axis, bit, one_way=False):
    count = lax.axis_size(axis)
    route = []
    for low in range(count):
        high = low | 1 << bit
        if high != low and high < count:
            route.append((low, high))
            if not one_way:
                route.append((high, low))
    return lax.ppermute(block, axis, route)


def to_offset(block, axis, offset):
    count = lax.axis_size(axis)
    return lax.ppermute(block, axis, [(s, s ^ offset) for s in range(count)])


def shards(queries, keys, values, mixing):
    rows = queries.shape[0]
    head_count = mixing.shape[1]
    dk = queries.shape[1] // head_count
    scale = dk ** (-0.5)
    level_count = (rows // SPAN).bit_length()
    mix_t = mixing.transpose(1, 2, 0)
    masks = jnp.asarray(level_masks(TQ, level_count))

    state = own_state(keys, values, head_count)

    seq_count = lax.axis_size("seq")
    ctx_count = lax.axis_size("ctx")
    seq_bits = seq_count.bit_length() - 1
    ctx_bits = ctx_count.bit_length() - 1
    seq_place = lax.axis_index("seq")
    ctx_place = lax.axis_index("ctx")

    sibs = []
    flags = []
    running = state
    half = head_count // 2
    for bit in range(seq_bits):
        if bit == 0 or seq_count < 4:
            partner = swap(running, "seq", bit)
        else:
            mine = seq_place & 1
            sent = lax.dynamic_slice_in_dim(running, mine * half, half, 0)
            got = swap(sent, "seq", bit)
            other = swap(got, "seq", 0)
            lo = jnp.where(mine == 0, got, other)
            hi = jnp.where(mine == 0, other, got)
            partner = jnp.concatenate([lo, hi], axis=0)
        sibs.append(partner)
        flags.append(seq_place >> bit & 1)
        running = running + partner

    share = head_count // seq_count
    quarter = lax.dynamic_slice_in_dim(running, seq_place * share, share, 0)
    ctx_sibs = []
    for bit in range(ctx_bits):
        got = swap(quarter, "ctx", bit, one_way=(bit == ctx_bits - 1))
        ctx_sibs.append(got)
        if bit != ctx_bits - 1:
            quarter = quarter + got

    for bit in range(ctx_bits):
        part = ctx_sibs[bit]
        parts = {0: part}
        for offset in range(1, seq_count):
            if offset & 1 and offset > 1:
                parts[offset] = to_offset(parts[offset ^ 1], "seq", 1)
            else:
                parts[offset] = to_offset(part, "seq", offset)
        full = []
        for owner in range(seq_count):
            pick = jnp.zeros_like(part)
            for offset in range(seq_count):
                pick = jnp.where((seq_place ^ offset) == owner, parts[offset], pick)
            full.append(pick)
        sibs.append(jnp.concatenate(full, axis=0))
        flags.append(ctx_place >> bit & 1)

    rounded = [
        (flags[i].astype(jnp.float32) * sibs[i]).astype(jnp.bfloat16) for i in range(len(sibs))
    ]
    early = jnp.stack(rounded[:-1])
    last = rounded[-1][None]

    per = head_count // CHUNKS
    local = None
    for c in range(CHUNKS):
        local = local_part(
            queries, keys, values, mix_t, masks, c * per, per, LOCAL_GROUP, scale, local
        )
    out = cross_all(queries, early, mix_t, local, scale, level_count, CROSS_GROUP)
    return cross_all(
        queries, last, mix_t, out, scale, level_count + len(rounded) - 1, CROSS_GROUP
    )


def solution(mesh):
    return jax.shard_map(
        shards,
        mesh=mesh,
        in_specs=(
            P(("ctx", "seq"), None),
            P(("ctx", "seq"), None),
            P(("ctx", "seq"), None),
            P(None, None, ("ctx", "seq")),
        ),
        out_specs=P(("ctx", "seq"), None),
        check_vma=False,
    )
```

```python
import functools

import numpy as np
import jax
import jax.numpy as jnp
from jax import lax
from jax.experimental import pallas as pl
from jax.experimental.pallas import tpu as pltpu
from jax.sharding import PartitionSpec as P

SPAN = 64
TQ = 256
CHUNKS = 4
LOCAL_GROUP = 2
CROSS_GROUP = 4


def level_masks(block, level_count):
    pos = np.arange(block)
    span = pos // SPAN
    crossed = span[:, None] ^ span[None, :]
    level = np.zeros_like(crossed)
    for power_index in range(level_count - 1):
        level = level + (crossed >= 2**power_index)
    causal = pos[:, None] >= pos[None, :]
    inner = int(np.log2(block // SPAN)) + 1
    return np.stack(
        [((level == l) & causal).astype(np.float32) for l in range(inner)]
    )


def state_kernel(head_count, k_ref, v_ref, o_ref):
    @pl.when(pl.program_id(0) == 0)
    def _():
        o_ref[...] = jnp.zeros_like(o_ref)

    dk = o_ref.shape[1]
    dv = o_ref.shape[2]
    for h in range(head_count):
        o_ref[h] += lax.dot_general(
            k_ref[:, h * dk:(h + 1) * dk], v_ref[:, h * dv:(h + 1) * dv],
            (((0,), (0,)), ((), ())), preferred_element_type=jnp.float32,
        )


def own_state(keys, values, head_count):
    rows, width = keys.shape
    dk = width // head_count
    dv = values.shape[1] // head_count
    tr = min(rows, 512)
    return pl.pallas_call(
        functools.partial(state_kernel, head_count),
        grid=(rows // tr,),
        in_specs=[
            pl.BlockSpec((tr, width), lambda r: (r, 0)),
            pl.BlockSpec((tr, values.shape[1]), lambda r: (r, 0)),
        ],
        out_specs=pl.BlockSpec((head_count, dk, dv), lambda r: (0, 0, 0)),
        out_shape=jax.ShapeDtypeStruct((head_count, dk, dv), jnp.float32),
        cost_estimate=pl.CostEstimate(
            flops=2 * rows * dk * dv * head_count,
            bytes_accessed=2 * rows * (dk + dv) * head_count + 4 * dk * dv * head_count,
            transcendentals=0,
        ),
        compiler_params=pltpu.CompilerParams(vmem_limit_bytes=64 * 1024 * 1024),
    )(keys, values)


def local_kernel(scale, rows, group, q_ref, k_ref, v_ref, m_ref, c_ref, *rest):
    o_ref = rest[-1]
    blocks = rows // TQ
    inner = c_ref.shape[0]
    dk = q_ref.shape[1] // group
    dv = v_ref.shape[1] // group
    for j in range(group):
        qc = slice(j * dk, (j + 1) * dk)
        vc = slice(j * dv, (j + 1) * dv)
        for a in range(blocks):
            r0 = a * TQ
            s = lax.dot_general(
                q_ref[r0:r0 + TQ, qc], k_ref[0:r0 + TQ, qc],
                (((1,), (1,)), ((), ())), preferred_element_type=jnp.float32,
            )
            s = s * scale
            mix = m_ref[j, :, r0:r0 + TQ].T
            pieces = []
            for b in range(a):
                level = inner + (a ^ b).bit_length() - 1
                w = mix[:, level:level + 1]
                pieces.append((s[:, b * TQ:(b + 1) * TQ] * w).astype(jnp.bfloat16))
            wd = c_ref[0] * mix[:, 0:1]
            for l in range(1, inner):
                wd = wd + c_ref[l] * mix[:, l:l + 1]
            pieces.append((s[:, r0:r0 + TQ] * wd).astype(jnp.bfloat16))
            p = pieces[0] if len(pieces) == 1 else jnp.concatenate(pieces, axis=1)
            o_ref[r0:r0 + TQ, vc] = jnp.dot(
                p, v_ref[0:r0 + TQ, vc], preferred_element_type=jnp.float32
            )


def local_part(queries, keys, values, mix_t, masks, first, count, group, scale, prev):
    rows = queries.shape[0]
    head_count = mix_t.shape[0]
    dk = queries.shape[1] // head_count
    dv = values.shape[1] // head_count
    levels = mix_t.shape[1]
    blocks = rows // TQ
    tiles = blocks * (blocks + 1) // 2
    base = first // group
    in_specs = [
        pl.BlockSpec((rows, dk * group), lambda h: (0, h + base)),
        pl.BlockSpec((rows, dk * group), lambda h: (0, h + base)),
        pl.BlockSpec((rows, dv * group), lambda h: (0, h + base)),
        pl.BlockSpec((group, levels, rows), lambda h: (h + base, 0, 0)),
        pl.BlockSpec(masks.shape, lambda h: (0, 0, 0)),
    ]
    operands = [queries, keys, values, mix_t, masks]
    aliases = {}
    if prev is not None:
        in_specs.append(pl.BlockSpec(memory_space=pl.ANY))
        operands.append(prev)
        aliases = {5: 0}
    return pl.pallas_call(
        functools.partial(local_kernel, scale, rows, group),
        grid=(count // group,),
        in_specs=in_specs,
        out_specs=pl.BlockSpec((rows, dv * group), lambda h: (0, h + base)),
        out_shape=jax.ShapeDtypeStruct((rows, dv * head_count), jnp.float32),
        input_output_aliases=aliases,
        cost_estimate=pl.CostEstimate(
            flops=2 * tiles * TQ * TQ * (dk + dv) * count,
            bytes_accessed=(2 * rows * (2 * dk + dv) + 4 * rows * dv) * count,
            transcendentals=0,
        ),
        compiler_params=pltpu.CompilerParams(vmem_limit_bytes=64 * 1024 * 1024),
    )(*operands)


def cross_kernel(scale, rows, first_level, group, q_ref, s_ref, m_ref, l_ref, o_ref):
    bits = s_ref.shape[0]
    dk = s_ref.shape[2]
    dv = s_ref.shape[3]
    for j in range(group):
        sib = jnp.concatenate([s_ref[b, j] for b in range(bits)], axis=1)
        for a in range(rows // TQ):
            r0 = a * TQ
            t = jnp.dot(
                q_ref[r0:r0 + TQ, j * dk:(j + 1) * dk], sib,
                preferred_element_type=jnp.float32,
            )
            mix = m_ref[j, :, r0:r0 + TQ].T
            cross = jnp.zeros((TQ, dv), jnp.float32)
            for b in range(bits):
                w = mix[:, first_level + b:first_level + b + 1] * scale
                cross = cross + w * t[:, b * dv:(b + 1) * dv]
            o_ref[r0:r0 + TQ, j * dv:(j + 1) * dv] = (
                l_ref[r0:r0 + TQ, j * dv:(j + 1) * dv] + cross
            )


def cross_all(queries, sibs, mix_t, local, scale, first_level, group):
    rows = queries.shape[0]
    head_count = mix_t.shape[0]
    dk = queries.shape[1] // head_count
    dv = sibs.shape[3]
    levels = mix_t.shape[1]
    bits = sibs.shape[0]
    return pl.pallas_call(
        functools.partial(cross_kernel, scale, rows, first_level, group),
        grid=(head_count // group,),
        in_specs=[
            pl.BlockSpec((rows, dk * group), lambda g: (0, g)),
            pl.BlockSpec((bits, group, dk, dv), lambda g: (0, g, 0, 0)),
            pl.BlockSpec((group, levels, rows), lambda g: (g, 0, 0)),
            pl.BlockSpec((rows, dv * group), lambda g: (0, g)),
        ],
        out_specs=pl.BlockSpec((rows, dv * group), lambda g: (0, g)),
        out_shape=jax.ShapeDtypeStruct((rows, dv * head_count), jnp.float32),
        input_output_aliases={3: 0},
        cost_estimate=pl.CostEstimate(
            flops=2 * rows * dk * dv * bits * head_count,
            bytes_accessed=(2 * rows * dk + 8 * rows * dv) * head_count,
            transcendentals=0,
        ),
        compiler_params=pltpu.CompilerParams(vmem_limit_bytes=64 * 1024 * 1024),
    )(queries, sibs, mix_t, local)


def swap(block, axis, bit, one_way=False):
    count = lax.axis_size(axis)
    route = []
    for low in range(count):
        high = low | 1 << bit
        if high != low and high < count:
            route.append((low, high))
            if not one_way:
                route.append((high, low))
    return lax.ppermute(block, axis, route)


def to_offset(block, axis, offset):
    count = lax.axis_size(axis)
    return lax.ppermute(block, axis, [(s, s ^ offset) for s in range(count)])


def shards(queries, keys, values, mixing):
    rows = queries.shape[0]
    head_count = mixing.shape[1]
    dk = queries.shape[1] // head_count
    scale = dk ** (-0.5)
    level_count = (rows // SPAN).bit_length()
    pad = -mixing.shape[0] % 8
    mix_t = jnp.pad(mixing, ((0, pad), (0, 0), (0, 0))).transpose(1, 0, 2)
    masks = jnp.asarray(level_masks(TQ, level_count))

    state = own_state(keys, values, head_count)

    seq_count = lax.axis_size("seq")
    ctx_count = lax.axis_size("ctx")
    seq_bits = seq_count.bit_length() - 1
    ctx_bits = ctx_count.bit_length() - 1
    seq_place = lax.axis_index("seq")
    ctx_place = lax.axis_index("ctx")

    sibs = []
    flags = []
    running = state
    half = head_count // 2
    for bit in range(seq_bits):
        if bit == 0 or seq_count < 4:
            partner = swap(running, "seq", bit)
        else:
            mine = seq_place & 1
            sent = lax.dynamic_slice_in_dim(running, mine * half, half, 0)
            got = swap(sent, "seq", bit)
            other = swap(got, "seq", 0)
            lo = jnp.where(mine == 0, got, other)
            hi = jnp.where(mine == 0, other, got)
            partner = jnp.concatenate([lo, hi], axis=0)
        sibs.append(partner)
        flags.append(seq_place >> bit & 1)
        running = running + partner

    share = head_count // seq_count
    quarter = lax.dynamic_slice_in_dim(running, seq_place * share, share, 0)
    ctx_sibs = []
    for bit in range(ctx_bits):
        got = swap(quarter, "ctx", bit, one_way=(bit == ctx_bits - 1))
        ctx_sibs.append(got)
        if bit != ctx_bits - 1:
            quarter = quarter + got

    for bit in range(ctx_bits):
        part = ctx_sibs[bit]
        parts = {0: part}
        for offset in range(1, seq_count):
            if offset & 1 and offset > 1:
                parts[offset] = to_offset(parts[offset ^ 1], "seq", 1)
            else:
                parts[offset] = to_offset(part, "seq", offset)
        full = []
        for owner in range(seq_count):
            pick = jnp.zeros_like(part)
            for offset in range(seq_count):
                pick = jnp.where((seq_place ^ offset) == owner, parts[offset], pick)
            full.append(pick)
        sibs.append(jnp.concatenate(full, axis=0))
        flags.append(ctx_place >> bit & 1)

    rounded = jnp.stack(
        [(flags[i].astype(jnp.float32) * sibs[i]).astype(jnp.bfloat16) for i in range(len(sibs))]
    )

    per = head_count // CHUNKS
    local = None
    for c in range(CHUNKS):
        local = local_part(
            queries, keys, values, mix_t, masks, c * per, per, LOCAL_GROUP, scale, local
        )
    return cross_all(queries, rounded, mix_t, local, scale, level_count, CROSS_GROUP)


def solution(mesh):
    return jax.shard_map(
        shards,
        mesh=mesh,
        in_specs=(
            P(("ctx", "seq"), None),
            P(("ctx", "seq"), None),
            P(("ctx", "seq"), None),
            P(None, None, ("ctx", "seq")),
        ),
        out_specs=P(("ctx", "seq"), None),
        check_vma=False,
    )
```

```python
import functools

import numpy as np
import jax
import jax.numpy as jnp
from jax import lax
from jax.experimental import pallas as pl
from jax.experimental.pallas import tpu as pltpu
from jax.sharding import PartitionSpec as P

SPAN = 64
TQ = 256
CHUNKS = 4
LOCAL_GROUP = 2
CROSS_GROUP = 4


def level_masks(block, level_count):
    pos = np.arange(block)
    span = pos // SPAN
    crossed = span[:, None] ^ span[None, :]
    level = np.zeros_like(crossed)
    for power_index in range(level_count - 1):
        level = level + (crossed >= 2**power_index)
    causal = pos[:, None] >= pos[None, :]
    inner = int(np.log2(block // SPAN)) + 1
    return np.stack(
        [((level == l) & causal).astype(np.float32) for l in range(inner)]
    )


def state_kernel(head_count, k_ref, v_ref, o_ref):
    @pl.when(pl.program_id(0) == 0)
    def _():
        o_ref[...] = jnp.zeros_like(o_ref)

    dk = o_ref.shape[1]
    dv = o_ref.shape[2]
    for h in range(head_count):
        o_ref[h] += lax.dot_general(
            k_ref[:, h * dk:(h + 1) * dk], v_ref[:, h * dv:(h + 1) * dv],
            (((0,), (0,)), ((), ())), preferred_element_type=jnp.float32,
        )


def own_state(keys, values, head_count):
    rows, width = keys.shape
    dk = width // head_count
    dv = values.shape[1] // head_count
    tr = min(rows, 512)
    return pl.pallas_call(
        functools.partial(state_kernel, head_count),
        grid=(rows // tr,),
        in_specs=[
            pl.BlockSpec((tr, width), lambda r: (r, 0)),
            pl.BlockSpec((tr, values.shape[1]), lambda r: (r, 0)),
        ],
        out_specs=pl.BlockSpec((head_count, dk, dv), lambda r: (0, 0, 0)),
        out_shape=jax.ShapeDtypeStruct((head_count, dk, dv), jnp.float32),
        cost_estimate=pl.CostEstimate(
            flops=2 * rows * dk * dv * head_count,
            bytes_accessed=2 * rows * (dk + dv) * head_count + 4 * dk * dv * head_count,
            transcendentals=0,
        ),
        compiler_params=pltpu.CompilerParams(vmem_limit_bytes=64 * 1024 * 1024),
    )(keys, values)


def local_kernel(scale, rows, group, q_ref, k_ref, v_ref, m_ref, c_ref, *rest):
    o_ref = rest[-1]
    blocks = rows // TQ
    inner = c_ref.shape[0]
    dk = q_ref.shape[1] // group
    dv = v_ref.shape[1] // group
    for j in range(group):
        qc = slice(j * dk, (j + 1) * dk)
        vc = slice(j * dv, (j + 1) * dv)
        for a in range(blocks):
            r0 = a * TQ
            s = lax.dot_general(
                q_ref[r0:r0 + TQ, qc], k_ref[0:r0 + TQ, qc],
                (((1,), (1,)), ((), ())), preferred_element_type=jnp.float32,
            )
            s = s * scale
            mix = m_ref[j, r0:r0 + TQ, :]
            pieces = []
            for b in range(a):
                level = inner + (a ^ b).bit_length() - 1
                w = mix[:, level:level + 1]
                pieces.append((s[:, b * TQ:(b + 1) * TQ] * w).astype(jnp.bfloat16))
            wd = c_ref[0] * mix[:, 0:1]
            for l in range(1, inner):
                wd = wd + c_ref[l] * mix[:, l:l + 1]
            pieces.append((s[:, r0:r0 + TQ] * wd).astype(jnp.bfloat16))
            p = pieces[0] if len(pieces) == 1 else jnp.concatenate(pieces, axis=1)
            o_ref[r0:r0 + TQ, vc] = jnp.dot(
                p, v_ref[0:r0 + TQ, vc], preferred_element_type=jnp.float32
            )


def local_part(queries, keys, values, mix_t, masks, first, count, group, scale, prev):
    rows = queries.shape[0]
    head_count = mix_t.shape[0]
    dk = queries.shape[1] // head_count
    dv = values.shape[1] // head_count
    levels = mix_t.shape[2]
    blocks = rows // TQ
    tiles = blocks * (blocks + 1) // 2
    base = first // group
    in_specs = [
        pl.BlockSpec((rows, dk * group), lambda h: (0, h + base)),
        pl.BlockSpec((rows, dk * group), lambda h: (0, h + base)),
        pl.BlockSpec((rows, dv * group), lambda h: (0, h + base)),
        pl.BlockSpec((group, rows, levels), lambda h: (h + base, 0, 0)),
        pl.BlockSpec(masks.shape, lambda h: (0, 0, 0)),
    ]
    operands = [queries, keys, values, mix_t, masks]
    aliases = {}
    if prev is not None:
        in_specs.append(pl.BlockSpec(memory_space=pl.ANY))
        operands.append(prev)
        aliases = {5: 0}
    return pl.pallas_call(
        functools.partial(local_kernel, scale, rows, group),
        grid=(count // group,),
        in_specs=in_specs,
        out_specs=pl.BlockSpec((rows, dv * group), lambda h: (0, h + base)),
        out_shape=jax.ShapeDtypeStruct((rows, dv * head_count), jnp.float32),
        input_output_aliases=aliases,
        cost_estimate=pl.CostEstimate(
            flops=2 * tiles * TQ * TQ * (dk + dv) * count,
            bytes_accessed=(2 * rows * (2 * dk + dv) + 4 * rows * dv) * count,
            transcendentals=0,
        ),
        compiler_params=pltpu.CompilerParams(vmem_limit_bytes=64 * 1024 * 1024),
    )(*operands)


def cross_kernel(scale, rows, first_level, group, q_ref, s_ref, m_ref, l_ref, o_ref):
    bits = s_ref.shape[0]
    dk = s_ref.shape[2]
    dv = s_ref.shape[3]
    for j in range(group):
        sib = jnp.concatenate([s_ref[b, j] for b in range(bits)], axis=1)
        for a in range(rows // TQ):
            r0 = a * TQ
            t = jnp.dot(
                q_ref[r0:r0 + TQ, j * dk:(j + 1) * dk], sib,
                preferred_element_type=jnp.float32,
            )
            mix = m_ref[j, r0:r0 + TQ, :]
            cross = jnp.zeros((TQ, dv), jnp.float32)
            for b in range(bits):
                w = mix[:, first_level + b:first_level + b + 1] * scale
                cross = cross + w * t[:, b * dv:(b + 1) * dv]
            o_ref[r0:r0 + TQ, j * dv:(j + 1) * dv] = (
                l_ref[r0:r0 + TQ, j * dv:(j + 1) * dv] + cross
            )


def cross_all(queries, sibs, mix_t, local, scale, first_level, group):
    rows = queries.shape[0]
    head_count = mix_t.shape[0]
    dk = queries.shape[1] // head_count
    dv = sibs.shape[3]
    levels = mix_t.shape[2]
    bits = sibs.shape[0]
    return pl.pallas_call(
        functools.partial(cross_kernel, scale, rows, first_level, group),
        grid=(head_count // group,),
        in_specs=[
            pl.BlockSpec((rows, dk * group), lambda g: (0, g)),
            pl.BlockSpec((bits, group, dk, dv), lambda g: (0, g, 0, 0)),
            pl.BlockSpec((group, rows, levels), lambda g: (g, 0, 0)),
            pl.BlockSpec((rows, dv * group), lambda g: (0, g)),
        ],
        out_specs=pl.BlockSpec((rows, dv * group), lambda g: (0, g)),
        out_shape=jax.ShapeDtypeStruct((rows, dv * head_count), jnp.float32),
        input_output_aliases={3: 0},
        cost_estimate=pl.CostEstimate(
            flops=2 * rows * dk * dv * bits * head_count,
            bytes_accessed=(2 * rows * dk + 8 * rows * dv) * head_count,
            transcendentals=0,
        ),
        compiler_params=pltpu.CompilerParams(vmem_limit_bytes=64 * 1024 * 1024),
    )(queries, sibs, mix_t, local)


def swap(block, axis, bit, one_way=False):
    count = lax.axis_size(axis)
    route = []
    for low in range(count):
        high = low | 1 << bit
        if high != low and high < count:
            route.append((low, high))
            if not one_way:
                route.append((high, low))
    return lax.ppermute(block, axis, route)


def to_offset(block, axis, offset):
    count = lax.axis_size(axis)
    return lax.ppermute(block, axis, [(s, s ^ offset) for s in range(count)])


def shards(queries, keys, values, mixing):
    rows = queries.shape[0]
    head_count = mixing.shape[1]
    dk = queries.shape[1] // head_count
    scale = dk ** (-0.5)
    level_count = (rows // SPAN).bit_length()
    mix_t = mixing.transpose(1, 2, 0)
    masks = jnp.asarray(level_masks(TQ, level_count))

    state = own_state(keys, values, head_count)

    seq_count = lax.axis_size("seq")
    ctx_count = lax.axis_size("ctx")
    seq_bits = seq_count.bit_length() - 1
    ctx_bits = ctx_count.bit_length() - 1
    seq_place = lax.axis_index("seq")
    ctx_place = lax.axis_index("ctx")

    sibs = []
    flags = []
    running = state
    half = head_count // 2
    for bit in range(seq_bits):
        if bit == 0 or seq_count < 4:
            partner = swap(running, "seq", bit)
        else:
            mine = seq_place & 1
            sent = lax.dynamic_slice_in_dim(running, mine * half, half, 0)
            got = swap(sent, "seq", bit)
            other = swap(got, "seq", 0)
            lo = jnp.where(mine == 0, got, other)
            hi = jnp.where(mine == 0, other, got)
            partner = jnp.concatenate([lo, hi], axis=0)
        sibs.append(partner)
        flags.append(seq_place >> bit & 1)
        running = running + partner

    share = head_count // seq_count
    quarter = lax.dynamic_slice_in_dim(running, seq_place * share, share, 0)
    ctx_sibs = []
    for bit in range(ctx_bits):
        got = swap(quarter, "ctx", bit, one_way=(bit == ctx_bits - 1))
        ctx_sibs.append(got)
        if bit != ctx_bits - 1:
            quarter = quarter + got

    for bit in range(ctx_bits):
        part = lax.optimization_barrier(ctx_sibs[bit])
        parts = {0: part}
        for offset in range(1, seq_count):
            if offset & 1 and offset > 1:
                parts[offset] = to_offset(parts[offset ^ 1], "seq", 1)
            else:
                parts[offset] = to_offset(part, "seq", offset)
        full = []
        for owner in range(seq_count):
            pick = jnp.zeros_like(part)
            for offset in range(seq_count):
                pick = jnp.where((seq_place ^ offset) == owner, parts[offset], pick)
            full.append(pick)
        sibs.append(jnp.concatenate(full, axis=0))
        flags.append(ctx_place >> bit & 1)

    rounded = jnp.stack(
        [(flags[i].astype(jnp.float32) * sibs[i]).astype(jnp.bfloat16) for i in range(len(sibs))]
    )

    per = head_count // CHUNKS
    local = None
    for c in range(CHUNKS):
        local = local_part(
            queries, keys, values, mix_t, masks, c * per, per, LOCAL_GROUP, scale, local
        )
    return cross_all(queries, rounded, mix_t, local, scale, level_count, CROSS_GROUP)


def solution(mesh):
    return jax.shard_map(
        shards,
        mesh=mesh,
        in_specs=(
            P(("ctx", "seq"), None),
            P(("ctx", "seq"), None),
            P(("ctx", "seq"), None),
            P(None, None, ("ctx", "seq")),
        ),
        out_specs=P(("ctx", "seq"), None),
        check_vma=False,
    )
```

```python
import functools

import numpy as np
import jax
import jax.numpy as jnp
from jax import lax
from jax.experimental import pallas as pl
from jax.experimental.pallas import tpu as pltpu
from jax.sharding import PartitionSpec as P

SPAN = 64
TQ = 256
CHUNKS = 4
LOCAL_GROUP = 2


def level_masks(block, level_count):
    pos = np.arange(block)
    span = pos // SPAN
    crossed = span[:, None] ^ span[None, :]
    level = np.zeros_like(crossed)
    for power_index in range(level_count - 1):
        level = level + (crossed >= 2**power_index)
    causal = pos[:, None] >= pos[None, :]
    inner = int(np.log2(block // SPAN)) + 1
    return np.stack(
        [((level == l) & causal).astype(np.float32) for l in range(inner)]
    )


def state_kernel(head_count, k_ref, v_ref, o_ref):
    @pl.when(pl.program_id(0) == 0)
    def _():
        o_ref[...] = jnp.zeros_like(o_ref)

    dk = o_ref.shape[1]
    dv = o_ref.shape[2]
    for h in range(head_count):
        o_ref[h] += lax.dot_general(
            k_ref[:, h * dk:(h + 1) * dk], v_ref[:, h * dv:(h + 1) * dv],
            (((0,), (0,)), ((), ())), preferred_element_type=jnp.float32,
        )


def own_state(keys, values, head_count):
    rows, width = keys.shape
    dk = width // head_count
    dv = values.shape[1] // head_count
    tr = min(rows, 512)
    return pl.pallas_call(
        functools.partial(state_kernel, head_count),
        grid=(rows // tr,),
        in_specs=[
            pl.BlockSpec((tr, width), lambda r: (r, 0)),
            pl.BlockSpec((tr, values.shape[1]), lambda r: (r, 0)),
        ],
        out_specs=pl.BlockSpec((head_count, dk, dv), lambda r: (0, 0, 0)),
        out_shape=jax.ShapeDtypeStruct((head_count, dk, dv), jnp.float32),
        cost_estimate=pl.CostEstimate(
            flops=2 * rows * dk * dv * head_count,
            bytes_accessed=2 * rows * (dk + dv) * head_count + 4 * dk * dv * head_count,
            transcendentals=0,
        ),
        compiler_params=pltpu.CompilerParams(vmem_limit_bytes=64 * 1024 * 1024),
    )(keys, values)


def local_kernel(scale, rows, group, q_ref, k_ref, v_ref, m_ref, c_ref, *rest):
    o_ref = rest[-1]
    blocks = rows // TQ
    inner = c_ref.shape[0]
    dk = q_ref.shape[1] // group
    dv = v_ref.shape[1] // group
    for j in range(group):
        qc = slice(j * dk, (j + 1) * dk)
        vc = slice(j * dv, (j + 1) * dv)
        for a in range(blocks):
            r0 = a * TQ
            s = lax.dot_general(
                q_ref[r0:r0 + TQ, qc], k_ref[0:r0 + TQ, qc],
                (((1,), (1,)), ((), ())), preferred_element_type=jnp.float32,
            )
            s = s * scale
            mix = m_ref[j, r0:r0 + TQ, :]
            pieces = []
            for b in range(a):
                level = inner + (a ^ b).bit_length() - 1
                w = mix[:, level:level + 1]
                pieces.append((s[:, b * TQ:(b + 1) * TQ] * w).astype(jnp.bfloat16))
            wd = c_ref[0] * mix[:, 0:1]
            for l in range(1, inner):
                wd = wd + c_ref[l] * mix[:, l:l + 1]
            pieces.append((s[:, r0:r0 + TQ] * wd).astype(jnp.bfloat16))
            p = pieces[0] if len(pieces) == 1 else jnp.concatenate(pieces, axis=1)
            o_ref[r0:r0 + TQ, vc] = jnp.dot(
                p, v_ref[0:r0 + TQ, vc], preferred_element_type=jnp.float32
            )


def local_part(queries, keys, values, mix_t, masks, first, count, group, scale, prev):
    rows = queries.shape[0]
    head_count = mix_t.shape[0]
    dk = queries.shape[1] // head_count
    dv = values.shape[1] // head_count
    levels = mix_t.shape[2]
    blocks = rows // TQ
    tiles = blocks * (blocks + 1) // 2
    base = first // group
    in_specs = [
        pl.BlockSpec((rows, dk * group), lambda h: (0, h + base)),
        pl.BlockSpec((rows, dk * group), lambda h: (0, h + base)),
        pl.BlockSpec((rows, dv * group), lambda h: (0, h + base)),
        pl.BlockSpec((group, rows, levels), lambda h: (h + base, 0, 0)),
        pl.BlockSpec(masks.shape, lambda h: (0, 0, 0)),
    ]
    operands = [queries, keys, values, mix_t, masks]
    aliases = {}
    if prev is not None:
        in_specs.append(pl.BlockSpec(memory_space=pl.ANY))
        operands.append(prev)
        aliases = {5: 0}
    return pl.pallas_call(
        functools.partial(local_kernel, scale, rows, group),
        grid=(count // group,),
        in_specs=in_specs,
        out_specs=pl.BlockSpec((rows, dv * group), lambda h: (0, h + base)),
        out_shape=jax.ShapeDtypeStruct((rows, dv * head_count), jnp.float32),
        input_output_aliases=aliases,
        cost_estimate=pl.CostEstimate(
            flops=2 * tiles * TQ * TQ * (dk + dv) * count,
            bytes_accessed=(2 * rows * (2 * dk + dv) + 4 * rows * dv) * count,
            transcendentals=0,
        ),
        compiler_params=pltpu.CompilerParams(vmem_limit_bytes=64 * 1024 * 1024),
    )(*operands)


def cross_kernel(scale, rows, first_level, group, n_seq, n_ctx, n_off, sp_ref, q_ref, m_ref, l_ref, *rest):
    o_ref = rest[-1]
    seq_refs = rest[:n_seq]
    part_refs = rest[n_seq:n_seq + n_ctx * n_off]
    bits = n_seq + n_ctx
    dv = l_ref.shape[1] // group
    dk = q_ref.shape[1] // group
    off = jnp.bitwise_xor(sp_ref[0], pl.program_id(0))
    for j in range(group):
        blocks = []
        for b in range(n_seq):
            blocks.append(seq_refs[b][j])
        for c in range(n_ctx):
            pick = part_refs[c * n_off][j]
            for o in range(1, n_off):
                pick = jnp.where(off == o, part_refs[c * n_off + o][j], pick)
            blocks.append(pick)
        sib = jnp.concatenate(
            [
                (sp_ref[1 + b].astype(jnp.float32) * blocks[b]).astype(jnp.bfloat16)
                for b in range(bits)
            ],
            axis=1,
        )
        for a in range(rows // TQ):
            r0 = a * TQ
            t = jnp.dot(
                q_ref[r0:r0 + TQ, j * dk:(j + 1) * dk], sib,
                preferred_element_type=jnp.float32,
            )
            mix = m_ref[j, r0:r0 + TQ, :]
            w_all = mix[:, first_level:first_level + bits] * scale
            cross = jnp.zeros((TQ, dv), jnp.float32)
            for b in range(bits):
                cross = cross + w_all[:, b:b + 1] * t[:, b * dv:(b + 1) * dv]
            o_ref[r0:r0 + TQ, j * dv:(j + 1) * dv] = (
                l_ref[r0:r0 + TQ, j * dv:(j + 1) * dv] + cross
            )


def cross_all(queries, scalars, seq_sibs, ctx_parts, mix_t, local, scale, first_level, group):
    rows = queries.shape[0]
    head_count = mix_t.shape[0]
    dk = queries.shape[1] // head_count
    dv = seq_sibs[0].shape[2] if seq_sibs else ctx_parts[0][0].shape[2]
    levels = mix_t.shape[2]
    n_seq = len(seq_sibs)
    n_ctx = len(ctx_parts)
    n_off = len(ctx_parts[0]) if ctx_parts else 1
    bits = n_seq + n_ctx
    in_specs = [
        pl.BlockSpec((rows, dk * group), lambda g, sp: (0, g)),
        pl.BlockSpec((group, rows, levels), lambda g, sp: (g, 0, 0)),
        pl.BlockSpec((rows, dv * group), lambda g, sp: (0, g)),
    ]
    operands = [queries, mix_t, local]
    for x in seq_sibs:
        in_specs.append(pl.BlockSpec((group, dk, dv), lambda g, sp: (g, 0, 0)))
        operands.append(x)
    for parts in ctx_parts:
        for x in parts:
            in_specs.append(pl.BlockSpec(x.shape, lambda g, sp: (0, 0, 0)))
            operands.append(x)
    return pl.pallas_call(
        functools.partial(cross_kernel, scale, rows, first_level, group, n_seq, n_ctx, n_off),
        grid_spec=pltpu.PrefetchScalarGridSpec(
            num_scalar_prefetch=1,
            grid=(head_count // group,),
            in_specs=in_specs,
            out_specs=pl.BlockSpec((rows, dv * group), lambda g, sp: (0, g)),
        ),
        out_shape=jax.ShapeDtypeStruct((rows, dv * head_count), jnp.float32),
        input_output_aliases={3: 0},
        cost_estimate=pl.CostEstimate(
            flops=2 * rows * dk * dv * bits * head_count,
            bytes_accessed=(2 * rows * dk + 8 * rows * dv) * head_count,
            transcendentals=0,
        ),
        compiler_params=pltpu.CompilerParams(vmem_limit_bytes=64 * 1024 * 1024),
    )(scalars, *operands)


def swap(block, axis, bit, one_way=False):
    count = lax.axis_size(axis)
    route = []
    for low in range(count):
        high = low | 1 << bit
        if high != low and high < count:
            route.append((low, high))
            if not one_way:
                route.append((high, low))
    return lax.ppermute(block, axis, route)


def to_offset(block, axis, offset):
    count = lax.axis_size(axis)
    return lax.ppermute(block, axis, [(s, s ^ offset) for s in range(count)])


def shards(queries, keys, values, mixing):
    rows = queries.shape[0]
    head_count = mixing.shape[1]
    dk = queries.shape[1] // head_count
    scale = dk ** (-0.5)
    level_count = (rows // SPAN).bit_length()
    mix_t = mixing.transpose(1, 2, 0)
    masks = jnp.asarray(level_masks(TQ, level_count))

    state = own_state(keys, values, head_count)

    seq_count = lax.axis_size("seq")
    ctx_count = lax.axis_size("ctx")
    seq_bits = seq_count.bit_length() - 1
    ctx_bits = ctx_count.bit_length() - 1
    seq_place = lax.axis_index("seq")
    ctx_place = lax.axis_index("ctx")

    sibs = []
    flags = []
    running = state
    half = head_count // 2
    for bit in range(seq_bits):
        if bit == 0 or seq_count < 4:
            partner = swap(running, "seq", bit)
        else:
            mine = seq_place & 1
            sent = lax.dynamic_slice_in_dim(running, mine * half, half, 0)
            got = swap(sent, "seq", bit)
            other = swap(got, "seq", 0)
            lo = jnp.where(mine == 0, got, other)
            hi = jnp.where(mine == 0, other, got)
            partner = jnp.concatenate([lo, hi], axis=0)
        sibs.append(partner)
        flags.append(seq_place >> bit & 1)
        running = running + partner

    share = head_count // seq_count
    quarter = lax.dynamic_slice_in_dim(running, seq_place * share, share, 0)
    ctx_sibs = []
    for bit in range(ctx_bits):
        got = swap(quarter, "ctx", bit, one_way=(bit == ctx_bits - 1))
        ctx_sibs.append(got)
        if bit != ctx_bits - 1:
            quarter = quarter + got

    ctx_parts = []
    for bit in range(ctx_bits):
        part = lax.optimization_barrier(ctx_sibs[bit])
        parts = {0: part}
        for offset in range(1, seq_count):
            if offset & 1 and offset > 1:
                parts[offset] = to_offset(parts[offset ^ 1], "seq", 1)
            else:
                parts[offset] = to_offset(part, "seq", offset)
        ctx_parts.append([parts[o] for o in range(seq_count)])
        flags.append(ctx_place >> bit & 1)
    scalars = jnp.stack([seq_place] + flags).astype(jnp.int32)

    per = head_count // CHUNKS
    local = None
    for c in range(CHUNKS):
        local = local_part(
            queries, keys, values, mix_t, masks, c * per, per, LOCAL_GROUP, scale, local
        )
    return cross_all(
        queries, scalars, sibs, ctx_parts, mix_t, local, scale, level_count,
        head_count // seq_count,
    )


def solution(mesh):
    return jax.shard_map(
        shards,
        mesh=mesh,
        in_specs=(
            P(("ctx", "seq"), None),
            P(("ctx", "seq"), None),
            P(("ctx", "seq"), None),
            P(None, None, ("ctx", "seq")),
        ),
        out_specs=P(("ctx", "seq"), None),
        check_vma=False,
    )
```

```python
import functools

import numpy as np
import jax
import jax.numpy as jnp
from jax import lax
from jax.experimental import pallas as pl
from jax.experimental.pallas import tpu as pltpu
from jax.sharding import PartitionSpec as P

SPAN = 64
TQ = 256
CHUNKS = 4
LOCAL_GROUP = 2
CROSS_GROUP = 4


def level_masks(block, level_count):
    pos = np.arange(block)
    span = pos // SPAN
    crossed = span[:, None] ^ span[None, :]
    level = np.zeros_like(crossed)
    for power_index in range(level_count - 1):
        level = level + (crossed >= 2**power_index)
    causal = pos[:, None] >= pos[None, :]
    inner = int(np.log2(block // SPAN)) + 1
    return np.stack(
        [((level == l) & causal).astype(np.float32) for l in range(inner)]
    )


def state_kernel(head_count, k_ref, v_ref, o_ref):
    @pl.when(pl.program_id(0) == 0)
    def _():
        o_ref[...] = jnp.zeros_like(o_ref)

    dk = o_ref.shape[1]
    dv = o_ref.shape[2]
    for h in range(head_count):
        o_ref[h] += lax.dot_general(
            k_ref[:, h * dk:(h + 1) * dk], v_ref[:, h * dv:(h + 1) * dv],
            (((0,), (0,)), ((), ())), preferred_element_type=jnp.float32,
        )


def own_state(keys, values, head_count):
    rows, width = keys.shape
    dk = width // head_count
    dv = values.shape[1] // head_count
    tr = min(rows, 512)
    return pl.pallas_call(
        functools.partial(state_kernel, head_count),
        grid=(rows // tr,),
        in_specs=[
            pl.BlockSpec((tr, width), lambda r: (r, 0)),
            pl.BlockSpec((tr, values.shape[1]), lambda r: (r, 0)),
        ],
        out_specs=pl.BlockSpec((head_count, dk, dv), lambda r: (0, 0, 0)),
        out_shape=jax.ShapeDtypeStruct((head_count, dk, dv), jnp.float32),
        cost_estimate=pl.CostEstimate(
            flops=2 * rows * dk * dv * head_count,
            bytes_accessed=2 * rows * (dk + dv) * head_count + 4 * dk * dv * head_count,
            transcendentals=0,
        ),
        compiler_params=pltpu.CompilerParams(vmem_limit_bytes=64 * 1024 * 1024),
    )(keys, values)


def local_kernel(scale, rows, group, first, head_count, steps, q_ref, k_ref, v_ref, m_ref, c_ref, *rest):
    o_ref = rest[-1]
    blocks = rows // TQ
    inner = c_ref.shape[0]
    dk = q_ref.shape[1] // group
    dv = v_ref.shape[1] // group

    def column(r0, level, head):
        c = level * head_count + head
        return m_ref[r0:r0 + TQ, c:c + 1]

    def body(step):
        for j in range(group):
            head = first + step * group + j
            qc = slice(j * dk, (j + 1) * dk)
            vc = slice(j * dv, (j + 1) * dv)
            for a in range(blocks):
                r0 = a * TQ
                s = lax.dot_general(
                    q_ref[r0:r0 + TQ, qc], k_ref[0:r0 + TQ, qc],
                    (((1,), (1,)), ((), ())), preferred_element_type=jnp.float32,
                )
                s = s * scale
                pieces = []
                for b in range(a):
                    level = inner + (a ^ b).bit_length() - 1
                    w = column(r0, level, head)
                    pieces.append((s[:, b * TQ:(b + 1) * TQ] * w).astype(jnp.bfloat16))
                wd = c_ref[0] * column(r0, 0, head)
                for l in range(1, inner):
                    wd = wd + c_ref[l] * column(r0, l, head)
                pieces.append((s[:, r0:r0 + TQ] * wd).astype(jnp.bfloat16))
                p = pieces[0] if len(pieces) == 1 else jnp.concatenate(pieces, axis=1)
                o_ref[r0:r0 + TQ, vc] = jnp.dot(
                    p, v_ref[0:r0 + TQ, vc], preferred_element_type=jnp.float32
                )

    for step in range(steps):
        pl.when(pl.program_id(0) == step)(functools.partial(body, step))


def local_part(queries, keys, values, mix_t, masks, first, count, group, scale, prev, head_count):
    rows = queries.shape[0]
    dk = queries.shape[1] // head_count
    dv = values.shape[1] // head_count
    blocks = rows // TQ
    tiles = blocks * (blocks + 1) // 2
    base = first // group
    in_specs = [
        pl.BlockSpec((rows, dk * group), lambda h: (0, h + base)),
        pl.BlockSpec((rows, dk * group), lambda h: (0, h + base)),
        pl.BlockSpec((rows, dv * group), lambda h: (0, h + base)),
        pl.BlockSpec(mix_t.shape, lambda h: (0, 0)),
        pl.BlockSpec(masks.shape, lambda h: (0, 0, 0)),
    ]
    operands = [queries, keys, values, mix_t, masks]
    aliases = {}
    if prev is not None:
        in_specs.append(pl.BlockSpec(memory_space=pl.ANY))
        operands.append(prev)
        aliases = {5: 0}
    return pl.pallas_call(
        functools.partial(local_kernel, scale, rows, group, first, head_count, count // group),
        grid=(count // group,),
        in_specs=in_specs,
        out_specs=pl.BlockSpec((rows, dv * group), lambda h: (0, h + base)),
        out_shape=jax.ShapeDtypeStruct((rows, dv * head_count), jnp.float32),
        input_output_aliases=aliases,
        cost_estimate=pl.CostEstimate(
            flops=2 * tiles * TQ * TQ * (dk + dv) * count,
            bytes_accessed=(2 * rows * (2 * dk + dv) + 4 * rows * dv) * count,
            transcendentals=0,
        ),
        compiler_params=pltpu.CompilerParams(vmem_limit_bytes=64 * 1024 * 1024),
    )(*operands)


def cross_kernel(scale, rows, first_level, group, q_ref, s_ref, m_ref, l_ref, o_ref):
    bits = s_ref.shape[0]
    dk = s_ref.shape[2]
    dv = s_ref.shape[3]
    for j in range(group):
        sib = jnp.concatenate([s_ref[b, j] for b in range(bits)], axis=1)
        for a in range(rows // TQ):
            r0 = a * TQ
            t = jnp.dot(
                q_ref[r0:r0 + TQ, j * dk:(j + 1) * dk], sib,
                preferred_element_type=jnp.float32,
            )
            mix = m_ref[j, :, r0:r0 + TQ].T
            cross = jnp.zeros((TQ, dv), jnp.float32)
            for b in range(bits):
                w = mix[:, first_level + b:first_level + b + 1] * scale
                cross = cross + w * t[:, b * dv:(b + 1) * dv]
            o_ref[r0:r0 + TQ, j * dv:(j + 1) * dv] = (
                l_ref[r0:r0 + TQ, j * dv:(j + 1) * dv] + cross
            )


def cross_all(queries, sibs, mix_t, local, scale, first_level, group):
    rows = queries.shape[0]
    head_count = mix_t.shape[0]
    dk = queries.shape[1] // head_count
    dv = sibs.shape[3]
    levels = mix_t.shape[1]
    bits = sibs.shape[0]
    return pl.pallas_call(
        functools.partial(cross_kernel, scale, rows, first_level, group),
        grid=(head_count // group,),
        in_specs=[
            pl.BlockSpec((rows, dk * group), lambda g: (0, g)),
            pl.BlockSpec((bits, group, dk, dv), lambda g: (0, g, 0, 0)),
            pl.BlockSpec((group, levels, rows), lambda g: (g, 0, 0)),
            pl.BlockSpec((rows, dv * group), lambda g: (0, g)),
        ],
        out_specs=pl.BlockSpec((rows, dv * group), lambda g: (0, g)),
        out_shape=jax.ShapeDtypeStruct((rows, dv * head_count), jnp.float32),
        input_output_aliases={3: 0},
        cost_estimate=pl.CostEstimate(
            flops=2 * rows * dk * dv * bits * head_count,
            bytes_accessed=(2 * rows * dk + 8 * rows * dv) * head_count,
            transcendentals=0,
        ),
        compiler_params=pltpu.CompilerParams(vmem_limit_bytes=64 * 1024 * 1024),
    )(queries, sibs, mix_t, local)


def swap(block, axis, bit, one_way=False):
    count = lax.axis_size(axis)
    route = []
    for low in range(count):
        high = low | 1 << bit
        if high != low and high < count:
            route.append((low, high))
            if not one_way:
                route.append((high, low))
    return lax.ppermute(block, axis, route)


def to_offset(block, axis, offset):
    count = lax.axis_size(axis)
    return lax.ppermute(block, axis, [(s, s ^ offset) for s in range(count)])


def shards(queries, keys, values, mixing):
    rows = queries.shape[0]
    head_count = mixing.shape[1]
    dk = queries.shape[1] // head_count
    scale = dk ** (-0.5)
    level_count = (rows // SPAN).bit_length()
    mix_t = mixing.reshape(-1, rows).T
    masks = jnp.asarray(level_masks(TQ, level_count))

    state = own_state(keys, values, head_count)

    seq_count = lax.axis_size("seq")
    ctx_count = lax.axis_size("ctx")
    seq_bits = seq_count.bit_length() - 1
    ctx_bits = ctx_count.bit_length() - 1
    seq_place = lax.axis_index("seq")
    ctx_place = lax.axis_index("ctx")

    sibs = []
    flags = []
    running = state
    half = head_count // 2
    for bit in range(seq_bits):
        if bit == 0 or seq_count < 4:
            partner = swap(running, "seq", bit)
        else:
            mine = seq_place & 1
            sent = lax.dynamic_slice_in_dim(running, mine * half, half, 0)
            got = swap(sent, "seq", bit)
            other = swap(got, "seq", 0)
            lo = jnp.where(mine == 0, got, other)
            hi = jnp.where(mine == 0, other, got)
            partner = jnp.concatenate([lo, hi], axis=0)
        sibs.append(partner)
        flags.append(seq_place >> bit & 1)
        running = running + partner

    share = head_count // seq_count
    quarter = lax.dynamic_slice_in_dim(running, seq_place * share, share, 0)
    ctx_sibs = []
    for bit in range(ctx_bits):
        got = swap(quarter, "ctx", bit, one_way=(bit == ctx_bits - 1))
        ctx_sibs.append(got)
        if bit != ctx_bits - 1:
            quarter = quarter + got

    for bit in range(ctx_bits):
        part = lax.optimization_barrier(ctx_sibs[bit])
        parts = {0: part}
        for offset in range(1, seq_count):
            if offset & 1 and offset > 1:
                parts[offset] = to_offset(parts[offset ^ 1], "seq", 1)
            else:
                parts[offset] = to_offset(part, "seq", offset)
        full = []
        for owner in range(seq_count):
            pick = jnp.zeros_like(part)
            for offset in range(seq_count):
                pick = jnp.where((seq_place ^ offset) == owner, parts[offset], pick)
            full.append(pick)
        sibs.append(jnp.concatenate(full, axis=0))
        flags.append(ctx_place >> bit & 1)

    rounded = jnp.stack(
        [(flags[i].astype(jnp.float32) * sibs[i]).astype(jnp.bfloat16) for i in range(len(sibs))]
    )

    per = head_count // CHUNKS
    local = None
    for c in range(CHUNKS):
        local = local_part(
            queries, keys, values, mix_t, masks, c * per, per, LOCAL_GROUP, scale, local,
            head_count,
        )
    pad = -mixing.shape[0] % 8
    mix_c = jnp.pad(mixing, ((0, pad), (0, 0), (0, 0))).transpose(1, 0, 2)
    return cross_all(queries, rounded, mix_c, local, scale, level_count, CROSS_GROUP)


def solution(mesh):
    return jax.shard_map(
        shards,
        mesh=mesh,
        in_specs=(
            P(("ctx", "seq"), None),
            P(("ctx", "seq"), None),
            P(("ctx", "seq"), None),
            P(None, None, ("ctx", "seq")),
        ),
        out_specs=P(("ctx", "seq"), None),
        check_vma=False,
    )
```

```python
import functools

import numpy as np
import jax
import jax.numpy as jnp
from jax import lax
from jax.experimental import pallas as pl
from jax.experimental.pallas import tpu as pltpu
from jax.sharding import PartitionSpec as P

SPAN = 64
TQ = 256
CHUNKS = 4
LOCAL_GROUP = 2
CROSS_GROUP = 4


def level_masks(block, level_count):
    pos = np.arange(block)
    span = pos // SPAN
    crossed = span[:, None] ^ span[None, :]
    level = np.zeros_like(crossed)
    for power_index in range(level_count - 1):
        level = level + (crossed >= 2**power_index)
    causal = pos[:, None] >= pos[None, :]
    inner = int(np.log2(block // SPAN)) + 1
    return np.stack(
        [((level == l) & causal).astype(np.float32) for l in range(inner)]
    )


def state_kernel(head_count, k_ref, v_ref, o_ref):
    @pl.when(pl.program_id(0) == 0)
    def _():
        o_ref[...] = jnp.zeros_like(o_ref)

    dk = o_ref.shape[1]
    dv = o_ref.shape[2]
    for h in range(head_count):
        o_ref[h] += lax.dot_general(
            k_ref[:, h * dk:(h + 1) * dk], v_ref[:, h * dv:(h + 1) * dv],
            (((0,), (0,)), ((), ())), preferred_element_type=jnp.float32,
        )


def own_state(keys, values, head_count):
    rows, width = keys.shape
    dk = width // head_count
    dv = values.shape[1] // head_count
    tr = min(rows, 512)
    return pl.pallas_call(
        functools.partial(state_kernel, head_count),
        grid=(rows // tr,),
        in_specs=[
            pl.BlockSpec((tr, width), lambda r: (r, 0)),
            pl.BlockSpec((tr, values.shape[1]), lambda r: (r, 0)),
        ],
        out_specs=pl.BlockSpec((head_count, dk, dv), lambda r: (0, 0, 0)),
        out_shape=jax.ShapeDtypeStruct((head_count, dk, dv), jnp.float32),
        cost_estimate=pl.CostEstimate(
            flops=2 * rows * dk * dv * head_count,
            bytes_accessed=2 * rows * (dk + dv) * head_count + 4 * dk * dv * head_count,
            transcendentals=0,
        ),
        compiler_params=pltpu.CompilerParams(vmem_limit_bytes=64 * 1024 * 1024),
    )(keys, values)


def local_kernel(scale, rows, group, q_ref, k_ref, v_ref, m_ref, c_ref, *rest):
    o_ref = rest[-1]
    blocks = rows // TQ
    inner = c_ref.shape[0]
    dk = q_ref.shape[1] // group
    dv = v_ref.shape[1] // group
    for j in range(group):
        qc = slice(j * dk, (j + 1) * dk)
        vc = slice(j * dv, (j + 1) * dv)
        for a in range(blocks):
            r0 = a * TQ
            s = lax.dot_general(
                q_ref[r0:r0 + TQ, qc], k_ref[0:r0 + TQ, qc],
                (((1,), (1,)), ((), ())), preferred_element_type=jnp.float32,
            )
            s = s * scale
            mix = m_ref[j, r0:r0 + TQ, :]
            pieces = []
            for b in range(a):
                level = inner + (a ^ b).bit_length() - 1
                w = mix[:, level:level + 1]
                pieces.append((s[:, b * TQ:(b + 1) * TQ] * w).astype(jnp.bfloat16))
            wd = c_ref[0] * mix[:, 0:1]
            for l in range(1, inner):
                wd = wd + c_ref[l] * mix[:, l:l + 1]
            pieces.append((s[:, r0:r0 + TQ] * wd).astype(jnp.bfloat16))
            p = pieces[0] if len(pieces) == 1 else jnp.concatenate(pieces, axis=1)
            o_ref[r0:r0 + TQ, vc] = jnp.dot(
                p, v_ref[0:r0 + TQ, vc], preferred_element_type=jnp.float32
            )


def local_part(queries, keys, values, mix_t, masks, first, count, group, scale, prev):
    rows = queries.shape[0]
    head_count = mix_t.shape[0]
    dk = queries.shape[1] // head_count
    dv = values.shape[1] // head_count
    levels = mix_t.shape[2]
    blocks = rows // TQ
    tiles = blocks * (blocks + 1) // 2
    base = first // group
    in_specs = [
        pl.BlockSpec((rows, dk * group), lambda h: (0, h + base)),
        pl.BlockSpec((rows, dk * group), lambda h: (0, h + base)),
        pl.BlockSpec((rows, dv * group), lambda h: (0, h + base)),
        pl.BlockSpec((group, rows, levels), lambda h: (h + base, 0, 0)),
        pl.BlockSpec(masks.shape, lambda h: (0, 0, 0)),
    ]
    operands = [queries, keys, values, mix_t, masks]
    aliases = {}
    if prev is not None:
        in_specs.append(pl.BlockSpec(memory_space=pl.ANY))
        operands.append(prev)
        aliases = {5: 0}
    return pl.pallas_call(
        functools.partial(local_kernel, scale, rows, group),
        grid=(count // group,),
        in_specs=in_specs,
        out_specs=pl.BlockSpec((rows, dv * group), lambda h: (0, h + base)),
        out_shape=jax.ShapeDtypeStruct((rows, dv * head_count), jnp.float32),
        input_output_aliases=aliases,
        cost_estimate=pl.CostEstimate(
            flops=2 * tiles * TQ * TQ * (dk + dv) * count,
            bytes_accessed=(2 * rows * (2 * dk + dv) + 4 * rows * dv) * count,
            transcendentals=0,
        ),
        compiler_params=pltpu.CompilerParams(vmem_limit_bytes=64 * 1024 * 1024),
    )(*operands)


def cross_kernel(scale, rows, first_level, group, q_ref, s_ref, m_ref, l_ref, o_ref):
    bits = s_ref.shape[0]
    dk = s_ref.shape[2]
    dv = s_ref.shape[3]
    for j in range(group):
        sib = jnp.concatenate([s_ref[b, j] for b in range(bits)], axis=1)
        for a in range(rows // TQ):
            r0 = a * TQ
            t = jnp.dot(
                q_ref[r0:r0 + TQ, j * dk:(j + 1) * dk], sib,
                preferred_element_type=jnp.float32,
            )
            w_all = m_ref[j, r0:r0 + TQ, first_level:first_level + bits] * scale
            cross = w_all[:, 0:1] * t[:, 0:dv]
            for b in range(1, bits):
                cross = cross + w_all[:, b:b + 1] * t[:, b * dv:(b + 1) * dv]
            o_ref[r0:r0 + TQ, j * dv:(j + 1) * dv] = (
                l_ref[r0:r0 + TQ, j * dv:(j + 1) * dv] + cross
            )


def cross_all(queries, sibs, mix_t, local, scale, first_level, group):
    rows = queries.shape[0]
    head_count = mix_t.shape[0]
    dk = queries.shape[1] // head_count
    dv = sibs.shape[3]
    levels = mix_t.shape[2]
    bits = sibs.shape[0]
    return pl.pallas_call(
        functools.partial(cross_kernel, scale, rows, first_level, group),
        grid=(head_count // group,),
        in_specs=[
            pl.BlockSpec((rows, dk * group), lambda g: (0, g)),
            pl.BlockSpec((bits, group, dk, dv), lambda g: (0, g, 0, 0)),
            pl.BlockSpec((group, rows, levels), lambda g: (g, 0, 0)),
            pl.BlockSpec((rows, dv * group), lambda g: (0, g)),
        ],
        out_specs=pl.BlockSpec((rows, dv * group), lambda g: (0, g)),
        out_shape=jax.ShapeDtypeStruct((rows, dv * head_count), jnp.float32),
        input_output_aliases={3: 0},
        cost_estimate=pl.CostEstimate(
            flops=2 * rows * dk * dv * bits * head_count,
            bytes_accessed=(2 * rows * dk + 8 * rows * dv) * head_count,
            transcendentals=0,
        ),
        compiler_params=pltpu.CompilerParams(vmem_limit_bytes=64 * 1024 * 1024),
    )(queries, sibs, mix_t, local)


def swap(block, axis, bit, one_way=False):
    count = lax.axis_size(axis)
    route = []
    for low in range(count):
        high = low | 1 << bit
        if high != low and high < count:
            route.append((low, high))
            if not one_way:
                route.append((high, low))
    return lax.ppermute(block, axis, route)


def to_offset(block, axis, offset):
    count = lax.axis_size(axis)
    return lax.ppermute(block, axis, [(s, s ^ offset) for s in range(count)])


def shards(queries, keys, values, mixing):
    rows = queries.shape[0]
    head_count = mixing.shape[1]
    dk = queries.shape[1] // head_count
    scale = dk ** (-0.5)
    level_count = (rows // SPAN).bit_length()
    mix_t = mixing.transpose(1, 2, 0)
    masks = jnp.asarray(level_masks(TQ, level_count))

    state = own_state(keys, values, head_count)

    seq_count = lax.axis_size("seq")
    ctx_count = lax.axis_size("ctx")
    seq_bits = seq_count.bit_length() - 1
    ctx_bits = ctx_count.bit_length() - 1
    seq_place = lax.axis_index("seq")
    ctx_place = lax.axis_index("ctx")

    sibs = []
    flags = []
    running = state
    half = head_count // 2
    for bit in range(seq_bits):
        if bit == 0 or seq_count < 4:
            partner = swap(running, "seq", bit)
        else:
            mine = seq_place & 1
            sent = lax.dynamic_slice_in_dim(running, mine * half, half, 0)
            got = swap(sent, "seq", bit)
            other = swap(got, "seq", 0)
            lo = jnp.where(mine == 0, got, other)
            hi = jnp.where(mine == 0, other, got)
            partner = jnp.concatenate([lo, hi], axis=0)
        sibs.append(partner)
        flags.append(seq_place >> bit & 1)
        running = running + partner

    share = head_count // seq_count
    quarter = lax.dynamic_slice_in_dim(running, seq_place * share, share, 0)
    ctx_sibs = []
    for bit in range(ctx_bits):
        got = swap(quarter, "ctx", bit, one_way=(bit == ctx_bits - 1))
        ctx_sibs.append(got)
        if bit != ctx_bits - 1:
            quarter = quarter + got

    for bit in range(ctx_bits):
        part = lax.optimization_barrier(ctx_sibs[bit])
        parts = {0: part}
        for offset in range(1, seq_count):
            if offset & 1 and offset > 1:
                parts[offset] = to_offset(parts[offset ^ 1], "seq", 1)
            else:
                parts[offset] = to_offset(part, "seq", offset)
        full = []
        for owner in range(seq_count):
            pick = jnp.zeros_like(part)
            for offset in range(seq_count):
                pick = jnp.where((seq_place ^ offset) == owner, parts[offset], pick)
            full.append(pick)
        sibs.append(jnp.concatenate(full, axis=0))
        flags.append(ctx_place >> bit & 1)

    rounded = jnp.stack(
        [(flags[i].astype(jnp.float32) * sibs[i]).astype(jnp.bfloat16) for i in range(len(sibs))]
    )

    per = head_count // CHUNKS
    local = None
    for c in range(CHUNKS):
        local = local_part(
            queries, keys, values, mix_t, masks, c * per, per, LOCAL_GROUP, scale, local
        )
    return cross_all(queries, rounded, mix_t, local, scale, level_count, CROSS_GROUP)


def solution(mesh):
    return jax.shard_map(
        shards,
        mesh=mesh,
        in_specs=(
            P(("ctx", "seq"), None),
            P(("ctx", "seq"), None),
            P(("ctx", "seq"), None),
            P(None, None, ("ctx", "seq")),
        ),
        out_specs=P(("ctx", "seq"), None),
        check_vma=False,
    )
```

```python
import functools

import numpy as np
import jax
import jax.numpy as jnp
from jax import lax
from jax.experimental import pallas as pl
from jax.experimental.pallas import tpu as pltpu
from jax.sharding import PartitionSpec as P

SPAN = 64
TQ = 256
CHUNKS = 4
LOCAL_GROUP = 2


def level_masks(block, level_count):
    pos = np.arange(block)
    span = pos // SPAN
    crossed = span[:, None] ^ span[None, :]
    level = np.zeros_like(crossed)
    for power_index in range(level_count - 1):
        level = level + (crossed >= 2**power_index)
    causal = pos[:, None] >= pos[None, :]
    inner = int(np.log2(block // SPAN)) + 1
    return np.stack(
        [((level == l) & causal).astype(np.float32) for l in range(inner)]
    )


def state_kernel(head_count, k_ref, v_ref, o_ref):
    @pl.when(pl.program_id(0) == 0)
    def _():
        o_ref[...] = jnp.zeros_like(o_ref)

    dk = o_ref.shape[1]
    dv = o_ref.shape[2]
    for h in range(head_count):
        o_ref[h] += lax.dot_general(
            k_ref[:, h * dk:(h + 1) * dk], v_ref[:, h * dv:(h + 1) * dv],
            (((0,), (0,)), ((), ())), preferred_element_type=jnp.float32,
        )


def own_state(keys, values, head_count):
    rows, width = keys.shape
    dk = width // head_count
    dv = values.shape[1] // head_count
    tr = min(rows, 512)
    return pl.pallas_call(
        functools.partial(state_kernel, head_count),
        grid=(rows // tr,),
        in_specs=[
            pl.BlockSpec((tr, width), lambda r: (r, 0)),
            pl.BlockSpec((tr, values.shape[1]), lambda r: (r, 0)),
        ],
        out_specs=pl.BlockSpec((head_count, dk, dv), lambda r: (0, 0, 0)),
        out_shape=jax.ShapeDtypeStruct((head_count, dk, dv), jnp.float32),
        cost_estimate=pl.CostEstimate(
            flops=2 * rows * dk * dv * head_count,
            bytes_accessed=2 * rows * (dk + dv) * head_count + 4 * dk * dv * head_count,
            transcendentals=0,
        ),
        compiler_params=pltpu.CompilerParams(vmem_limit_bytes=64 * 1024 * 1024),
    )(keys, values)


def local_kernel(scale, rows, group, q_ref, k_ref, v_ref, m_ref, c_ref, *rest):
    o_ref = rest[-1]
    blocks = rows // TQ
    inner = c_ref.shape[0]
    dk = q_ref.shape[1] // group
    dv = v_ref.shape[1] // group
    for j in range(group):
        qc = slice(j * dk, (j + 1) * dk)
        vc = slice(j * dv, (j + 1) * dv)
        for a in range(blocks):
            r0 = a * TQ
            s = lax.dot_general(
                q_ref[r0:r0 + TQ, qc], k_ref[0:r0 + TQ, qc],
                (((1,), (1,)), ((), ())), preferred_element_type=jnp.float32,
            )
            s = s * scale
            mix = m_ref[j, r0:r0 + TQ, :]
            pieces = []
            for b in range(a):
                level = inner + (a ^ b).bit_length() - 1
                w = mix[:, level:level + 1]
                pieces.append((s[:, b * TQ:(b + 1) * TQ] * w).astype(jnp.bfloat16))
            wd = c_ref[0] * mix[:, 0:1]
            for l in range(1, inner):
                wd = wd + c_ref[l] * mix[:, l:l + 1]
            pieces.append((s[:, r0:r0 + TQ] * wd).astype(jnp.bfloat16))
            p = pieces[0] if len(pieces) == 1 else jnp.concatenate(pieces, axis=1)
            o_ref[r0:r0 + TQ, vc] = jnp.dot(
                p, v_ref[0:r0 + TQ, vc], preferred_element_type=jnp.float32
            )


def local_part(queries, keys, values, mix_t, masks, first, count, group, scale, prev):
    rows = queries.shape[0]
    head_count = mix_t.shape[0]
    dk = queries.shape[1] // head_count
    dv = values.shape[1] // head_count
    levels = mix_t.shape[2]
    blocks = rows // TQ
    tiles = blocks * (blocks + 1) // 2
    base = first // group
    in_specs = [
        pl.BlockSpec((rows, dk * group), lambda h: (0, h + base)),
        pl.BlockSpec((rows, dk * group), lambda h: (0, h + base)),
        pl.BlockSpec((rows, dv * group), lambda h: (0, h + base)),
        pl.BlockSpec((group, rows, levels), lambda h: (h + base, 0, 0)),
        pl.BlockSpec(masks.shape, lambda h: (0, 0, 0)),
    ]
    operands = [queries, keys, values, mix_t, masks]
    aliases = {}
    if prev is not None:
        in_specs.append(pl.BlockSpec(memory_space=pl.ANY))
        operands.append(prev)
        aliases = {5: 0}
    return pl.pallas_call(
        functools.partial(local_kernel, scale, rows, group),
        grid=(count // group,),
        in_specs=in_specs,
        out_specs=pl.BlockSpec((rows, dv * group), lambda h: (0, h + base)),
        out_shape=jax.ShapeDtypeStruct((rows, dv * head_count), jnp.float32),
        input_output_aliases=aliases,
        cost_estimate=pl.CostEstimate(
            flops=2 * tiles * TQ * TQ * (dk + dv) * count,
            bytes_accessed=(2 * rows * (2 * dk + dv) + 4 * rows * dv) * count,
            transcendentals=0,
        ),
        compiler_params=pltpu.CompilerParams(vmem_limit_bytes=64 * 1024 * 1024),
    )(*operands)


def cross2_kernel(scale, rows, first_level, group, sp_ref, q_ref, e_ref, t_ref, m_ref, l_ref, o_ref):
    bits = e_ref.shape[0] + 1
    dk = e_ref.shape[2]
    dv = e_ref.shape[3]
    for j in range(group):
        sib = jnp.concatenate(
            [e_ref[b, j] for b in range(bits - 1)] + [t_ref[0, j]], axis=1
        )
        for a in range(rows // TQ):
            r0 = a * TQ
            t = jnp.dot(
                q_ref[r0:r0 + TQ, j * dk:(j + 1) * dk], sib,
                preferred_element_type=jnp.float32,
            )
            w_all = m_ref[j, r0:r0 + TQ, first_level:first_level + bits] * scale
            cross = w_all[:, 0:1] * t[:, 0:dv]
            for b in range(1, bits):
                cross = cross + w_all[:, b:b + 1] * t[:, b * dv:(b + 1) * dv]
            o_ref[r0:r0 + TQ, j * dv:(j + 1) * dv] = (
                l_ref[r0:r0 + TQ, j * dv:(j + 1) * dv] + cross
            )


def cross_part2(queries, scalars, early, lastx, mix_t, prev, scale, first_level, group, base):
    rows = queries.shape[0]
    head_count = mix_t.shape[0]
    dk = queries.shape[1] // head_count
    dv = early.shape[3]
    levels = mix_t.shape[2]
    bits = early.shape[0] + 1
    steps = lastx.shape[1] // group

    def quarter(g, sp):
        return jnp.bitwise_xor(sp[0], g + base)

    return pl.pallas_call(
        functools.partial(cross2_kernel, scale, rows, first_level, group),
        grid_spec=pltpu.PrefetchScalarGridSpec(
            num_scalar_prefetch=1,
            grid=(steps,),
            in_specs=[
                pl.BlockSpec((rows, dk * group), lambda g, sp: (0, quarter(g, sp))),
                pl.BlockSpec((bits - 1, group, dk, dv), lambda g, sp: (0, quarter(g, sp), 0, 0)),
                pl.BlockSpec((1, group, dk, dv), lambda g, sp: (0, g, 0, 0)),
                pl.BlockSpec((group, rows, levels), lambda g, sp: (quarter(g, sp), 0, 0)),
                pl.BlockSpec((rows, dv * group), lambda g, sp: (0, quarter(g, sp))),
            ],
            out_specs=pl.BlockSpec((rows, dv * group), lambda g, sp: (0, quarter(g, sp))),
        ),
        out_shape=jax.ShapeDtypeStruct((rows, dv * head_count), jnp.float32),
        input_output_aliases={5: 0},
        cost_estimate=pl.CostEstimate(
            flops=2 * rows * dk * dv * bits * group * steps,
            bytes_accessed=(2 * rows * dk + 8 * rows * dv) * group * steps,
            transcendentals=0,
        ),
        compiler_params=pltpu.CompilerParams(vmem_limit_bytes=64 * 1024 * 1024),
    )(scalars, queries, early, lastx, mix_t, prev)


def swap(block, axis, bit, one_way=False):
    count = lax.axis_size(axis)
    route = []
    for low in range(count):
        high = low | 1 << bit
        if high != low and high < count:
            route.append((low, high))
            if not one_way:
                route.append((high, low))
    return lax.ppermute(block, axis, route)


def to_offset(block, axis, offset):
    count = lax.axis_size(axis)
    return lax.ppermute(block, axis, [(s, s ^ offset) for s in range(count)])


def shards(queries, keys, values, mixing):
    rows = queries.shape[0]
    head_count = mixing.shape[1]
    dk = queries.shape[1] // head_count
    scale = dk ** (-0.5)
    level_count = (rows // SPAN).bit_length()
    mix_t = mixing.transpose(1, 2, 0)
    masks = jnp.asarray(level_masks(TQ, level_count))

    state = own_state(keys, values, head_count)

    seq_count = lax.axis_size("seq")
    ctx_count = lax.axis_size("ctx")
    seq_bits = seq_count.bit_length() - 1
    ctx_bits = ctx_count.bit_length() - 1
    seq_place = lax.axis_index("seq")
    ctx_place = lax.axis_index("ctx")

    sibs = []
    flags = []
    running = state
    half = head_count // 2
    for bit in range(seq_bits):
        if bit == 0 or seq_count < 4:
            partner = swap(running, "seq", bit)
        else:
            mine = seq_place & 1
            sent = lax.dynamic_slice_in_dim(running, mine * half, half, 0)
            got = swap(sent, "seq", bit)
            other = swap(got, "seq", 0)
            lo = jnp.where(mine == 0, got, other)
            hi = jnp.where(mine == 0, other, got)
            partner = jnp.concatenate([lo, hi], axis=0)
        sibs.append(partner)
        flags.append(seq_place >> bit & 1)
        running = running + partner

    share = head_count // seq_count
    quarter = lax.dynamic_slice_in_dim(running, seq_place * share, share, 0)
    ctx_sibs = []
    for bit in range(ctx_bits):
        got = swap(quarter, "ctx", bit, one_way=(bit == ctx_bits - 1))
        ctx_sibs.append(got)
        if bit != ctx_bits - 1:
            quarter = quarter + got

    gathered = []
    for bit in range(ctx_bits):
        part = lax.optimization_barrier(ctx_sibs[bit])
        parts = {0: part}
        for offset in range(1, seq_count):
            if offset & 1 and offset > 1:
                parts[offset] = to_offset(parts[offset ^ 1], "seq", 1)
            else:
                parts[offset] = to_offset(part, "seq", offset)
        gathered.append(parts)
        flags.append(ctx_place >> bit & 1)
    for bit in range(ctx_bits - 1):
        parts = gathered[bit]
        full = []
        for owner in range(seq_count):
            pick = jnp.zeros_like(parts[0])
            for offset in range(seq_count):
                pick = jnp.where((seq_place ^ offset) == owner, parts[offset], pick)
            full.append(pick)
        sibs.append(jnp.concatenate(full, axis=0))

    early = jnp.stack(
        [(flags[i].astype(jnp.float32) * sibs[i]).astype(jnp.bfloat16) for i in range(len(sibs))]
    )
    last_flag = flags[-1].astype(jnp.float32)
    last_parts = gathered[-1]
    split = seq_count // 2
    share = head_count // seq_count

    def last_of(offsets):
        picked = [(last_flag * last_parts[o]).astype(jnp.bfloat16) for o in offsets]
        return jnp.concatenate(picked, axis=0)[None]

    last_a = last_of(range(split))
    last_b = last_of(range(split, seq_count))
    scalars = seq_place.astype(jnp.int32)[None]

    per = head_count // CHUNKS
    local = None
    for c in range(CHUNKS):
        local = local_part(
            queries, keys, values, mix_t, masks, c * per, per, LOCAL_GROUP, scale, local
        )
    out = cross_part2(queries, scalars, early, last_a, mix_t, local, scale, level_count, share, 0)
    return cross_part2(
        queries, scalars, early, last_b, mix_t, out, scale, level_count, share, split
    )


def solution(mesh):
    return jax.shard_map(
        shards,
        mesh=mesh,
        in_specs=(
            P(("ctx", "seq"), None),
            P(("ctx", "seq"), None),
            P(("ctx", "seq"), None),
            P(None, None, ("ctx", "seq")),
        ),
        out_specs=P(("ctx", "seq"), None),
        check_vma=False,
    )
```

```python
import functools

import numpy as np
import jax
import jax.numpy as jnp
from jax import lax
from jax.experimental import pallas as pl
from jax.experimental.pallas import tpu as pltpu
from jax.sharding import PartitionSpec as P

SPAN = 64
TQ = 256
CHUNKS = 4
LOCAL_GROUP = 2
CROSS_GROUP = 4


def level_masks(block, level_count):
    pos = np.arange(block)
    span = pos // SPAN
    crossed = span[:, None] ^ span[None, :]
    level = np.zeros_like(crossed)
    for power_index in range(level_count - 1):
        level = level + (crossed >= 2**power_index)
    causal = pos[:, None] >= pos[None, :]
    inner = int(np.log2(block // SPAN)) + 1
    return np.stack(
        [((level == l) & causal).astype(np.float32) for l in range(inner)]
    )


def state_kernel(head_count, k_ref, v_ref, o_ref):
    @pl.when(pl.program_id(0) == 0)
    def _():
        o_ref[...] = jnp.zeros_like(o_ref)

    dk = o_ref.shape[1]
    dv = o_ref.shape[2]
    for h in range(head_count):
        o_ref[h] += lax.dot_general(
            k_ref[:, h * dk:(h + 1) * dk], v_ref[:, h * dv:(h + 1) * dv],
            (((0,), (0,)), ((), ())), preferred_element_type=jnp.float32,
        )


def own_state(keys, values, head_count):
    rows, width = keys.shape
    dk = width // head_count
    dv = values.shape[1] // head_count
    tr = min(rows, 512)
    return pl.pallas_call(
        functools.partial(state_kernel, head_count),
        grid=(rows // tr,),
        in_specs=[
            pl.BlockSpec((tr, width), lambda r: (r, 0)),
            pl.BlockSpec((tr, values.shape[1]), lambda r: (r, 0)),
        ],
        out_specs=pl.BlockSpec((head_count, dk, dv), lambda r: (0, 0, 0)),
        out_shape=jax.ShapeDtypeStruct((head_count, dk, dv), jnp.float32),
        cost_estimate=pl.CostEstimate(
            flops=2 * rows * dk * dv * head_count,
            bytes_accessed=2 * rows * (dk + dv) * head_count + 4 * dk * dv * head_count,
            transcendentals=0,
        ),
        compiler_params=pltpu.CompilerParams(vmem_limit_bytes=64 * 1024 * 1024),
    )(keys, values)


def local_kernel(scale, rows, group, levels, q_ref, k_ref, v_ref, m_ref, c_ref, *rest):
    o_ref = rest[-1]
    blocks = rows // TQ
    inner = c_ref.shape[0]
    dk = q_ref.shape[1] // group
    dv = v_ref.shape[1] // group
    for j in range(group):
        qc = slice(j * dk, (j + 1) * dk)
        vc = slice(j * dv, (j + 1) * dv)
        for a in range(blocks):
            r0 = a * TQ
            s = lax.dot_general(
                q_ref[r0:r0 + TQ, qc], k_ref[0:r0 + TQ, qc],
                (((1,), (1,)), ((), ())), preferred_element_type=jnp.float32,
            )
            s = s * scale
            mix = m_ref[r0:r0 + TQ, j * levels:(j + 1) * levels]
            pieces = []
            for b in range(a):
                level = inner + (a ^ b).bit_length() - 1
                w = mix[:, level:level + 1]
                pieces.append((s[:, b * TQ:(b + 1) * TQ] * w).astype(jnp.bfloat16))
            wd = c_ref[0] * mix[:, 0:1]
            for l in range(1, inner):
                wd = wd + c_ref[l] * mix[:, l:l + 1]
            pieces.append((s[:, r0:r0 + TQ] * wd).astype(jnp.bfloat16))
            p = pieces[0] if len(pieces) == 1 else jnp.concatenate(pieces, axis=1)
            o_ref[r0:r0 + TQ, vc] = jnp.dot(
                p, v_ref[0:r0 + TQ, vc], preferred_element_type=jnp.float32
            )


def local_part(queries, keys, values, mix_t, masks, first, count, group, scale, prev, head_count, levels):
    rows = queries.shape[0]
    dk = queries.shape[1] // head_count
    dv = values.shape[1] // head_count
    blocks = rows // TQ
    tiles = blocks * (blocks + 1) // 2
    base = first // group
    in_specs = [
        pl.BlockSpec((rows, dk * group), lambda h: (0, h + base)),
        pl.BlockSpec((rows, dk * group), lambda h: (0, h + base)),
        pl.BlockSpec((rows, dv * group), lambda h: (0, h + base)),
        pl.BlockSpec((rows, 128), lambda h: (0, h + base)),
        pl.BlockSpec(masks.shape, lambda h: (0, 0, 0)),
    ]
    operands = [queries, keys, values, mix_t, masks]
    aliases = {}
    if prev is not None:
        in_specs.append(pl.BlockSpec(memory_space=pl.ANY))
        operands.append(prev)
        aliases = {5: 0}
    return pl.pallas_call(
        functools.partial(local_kernel, scale, rows, group, levels),
        grid=(count // group,),
        in_specs=in_specs,
        out_specs=pl.BlockSpec((rows, dv * group), lambda h: (0, h + base)),
        out_shape=jax.ShapeDtypeStruct((rows, dv * head_count), jnp.float32),
        input_output_aliases=aliases,
        cost_estimate=pl.CostEstimate(
            flops=2 * tiles * TQ * TQ * (dk + dv) * count,
            bytes_accessed=(2 * rows * (2 * dk + dv) + 4 * rows * dv) * count,
            transcendentals=0,
        ),
        compiler_params=pltpu.CompilerParams(vmem_limit_bytes=64 * 1024 * 1024),
    )(*operands)


def cross_kernel(scale, rows, first_level, group, levels, q_ref, s_ref, m_ref, l_ref, o_ref):
    bits = s_ref.shape[0]
    dk = s_ref.shape[2]
    dv = s_ref.shape[3]
    for j in range(group):
        sib = jnp.concatenate([s_ref[b, j] for b in range(bits)], axis=1)
        for a in range(rows // TQ):
            r0 = a * TQ
            t = jnp.dot(
                q_ref[r0:r0 + TQ, j * dk:(j + 1) * dk], sib,
                preferred_element_type=jnp.float32,
            )
            c0 = (j // 2) * 128 + (j % 2) * levels + first_level
            w_all = m_ref[r0:r0 + TQ, c0:c0 + bits] * scale
            cross = w_all[:, 0:1] * t[:, 0:dv]
            for b in range(1, bits):
                cross = cross + w_all[:, b:b + 1] * t[:, b * dv:(b + 1) * dv]
            o_ref[r0:r0 + TQ, j * dv:(j + 1) * dv] = (
                l_ref[r0:r0 + TQ, j * dv:(j + 1) * dv] + cross
            )


def cross_all(queries, sibs, mix_t, local, scale, first_level, group, head_count, levels):
    rows = queries.shape[0]
    dk = queries.shape[1] // head_count
    dv = sibs.shape[3]
    bits = sibs.shape[0]
    return pl.pallas_call(
        functools.partial(cross_kernel, scale, rows, first_level, group, levels),
        grid=(head_count // group,),
        in_specs=[
            pl.BlockSpec((rows, dk * group), lambda g: (0, g)),
            pl.BlockSpec((bits, group, dk, dv), lambda g: (0, g, 0, 0)),
            pl.BlockSpec((rows, 128 * group // 2), lambda g: (0, g)),
            pl.BlockSpec((rows, dv * group), lambda g: (0, g)),
        ],
        out_specs=pl.BlockSpec((rows, dv * group), lambda g: (0, g)),
        out_shape=jax.ShapeDtypeStruct((rows, dv * head_count), jnp.float32),
        input_output_aliases={3: 0},
        cost_estimate=pl.CostEstimate(
            flops=2 * rows * dk * dv * bits * head_count,
            bytes_accessed=(2 * rows * dk + 8 * rows * dv) * head_count,
            transcendentals=0,
        ),
        compiler_params=pltpu.CompilerParams(vmem_limit_bytes=64 * 1024 * 1024),
    )(queries, sibs, mix_t, local)


def swap(block, axis, bit, one_way=False):
    count = lax.axis_size(axis)
    route = []
    for low in range(count):
        high = low | 1 << bit
        if high != low and high < count:
            route.append((low, high))
            if not one_way:
                route.append((high, low))
    return lax.ppermute(block, axis, route)


def to_offset(block, axis, offset):
    count = lax.axis_size(axis)
    return lax.ppermute(block, axis, [(s, s ^ offset) for s in range(count)])


def shards(queries, keys, values, mixing):
    rows = queries.shape[0]
    head_count = mixing.shape[1]
    dk = queries.shape[1] // head_count
    scale = dk ** (-0.5)
    level_count = (rows // SPAN).bit_length()
    levels = mixing.shape[0]
    paired = mixing.reshape(levels, head_count // 2, 2, rows).transpose(3, 1, 2, 0)
    paired = paired.reshape(rows, head_count // 2, 2 * levels)
    mix_t = jnp.pad(paired, ((0, 0), (0, 0), (0, 128 - 2 * levels))).reshape(rows, -1)
    masks = jnp.asarray(level_masks(TQ, level_count))

    state = own_state(keys, values, head_count)

    seq_count = lax.axis_size("seq")
    ctx_count = lax.axis_size("ctx")
    seq_bits = seq_count.bit_length() - 1
    ctx_bits = ctx_count.bit_length() - 1
    seq_place = lax.axis_index("seq")
    ctx_place = lax.axis_index("ctx")

    sibs = []
    flags = []
    running = state
    half = head_count // 2
    for bit in range(seq_bits):
        if bit == 0 or seq_count < 4:
            partner = swap(running, "seq", bit)
        else:
            mine = seq_place & 1
            sent = lax.dynamic_slice_in_dim(running, mine * half, half, 0)
            got = swap(sent, "seq", bit)
            other = swap(got, "seq", 0)
            lo = jnp.where(mine == 0, got, other)
            hi = jnp.where(mine == 0, other, got)
            partner = jnp.concatenate([lo, hi], axis=0)
        sibs.append(partner)
        flags.append(seq_place >> bit & 1)
        running = running + partner

    share = head_count // seq_count
    quarter = lax.dynamic_slice_in_dim(running, seq_place * share, share, 0)
    ctx_sibs = []
    for bit in range(ctx_bits):
        got = swap(quarter, "ctx", bit, one_way=(bit == ctx_bits - 1))
        ctx_sibs.append(got)
        if bit != ctx_bits - 1:
            quarter = quarter + got

    for bit in range(ctx_bits):
        part = lax.optimization_barrier(ctx_sibs[bit])
        parts = {0: part}
        for offset in range(1, seq_count):
            if offset & 1 and offset > 1:
                parts[offset] = to_offset(parts[offset ^ 1], "seq", 1)
            else:
                parts[offset] = to_offset(part, "seq", offset)
        full = []
        for owner in range(seq_count):
            pick = jnp.zeros_like(part)
            for offset in range(seq_count):
                pick = jnp.where((seq_place ^ offset) == owner, parts[offset], pick)
            full.append(pick)
        sibs.append(jnp.concatenate(full, axis=0))
        flags.append(ctx_place >> bit & 1)

    rounded = jnp.stack(
        [(flags[i].astype(jnp.float32) * sibs[i]).astype(jnp.bfloat16) for i in range(len(sibs))]
    )

    per = head_count // CHUNKS
    local = None
    for c in range(CHUNKS):
        local = local_part(
            queries, keys, values, mix_t, masks, c * per, per, LOCAL_GROUP, scale, local,
            head_count, levels,
        )
    return cross_all(
        queries, rounded, mix_t, local, scale, level_count, CROSS_GROUP, head_count, levels
    )


def solution(mesh):
    return jax.shard_map(
        shards,
        mesh=mesh,
        in_specs=(
            P(("ctx", "seq"), None),
            P(("ctx", "seq"), None),
            P(("ctx", "seq"), None),
            P(None, None, ("ctx", "seq")),
        ),
        out_specs=P(("ctx", "seq"), None),
        check_vma=False,
    )
```

```python
import functools

import numpy as np
import jax
import jax.numpy as jnp
from jax import lax
from jax.experimental import pallas as pl
from jax.experimental.pallas import tpu as pltpu
from jax.sharding import PartitionSpec as P

SPAN = 64
TQ = 256
CHUNKS = 4
LOCAL_GROUP = 2
CROSS_GROUP = 4


def level_masks(block, level_count):
    pos = np.arange(block)
    span = pos // SPAN
    crossed = span[:, None] ^ span[None, :]
    level = np.zeros_like(crossed)
    for power_index in range(level_count - 1):
        level = level + (crossed >= 2**power_index)
    causal = pos[:, None] >= pos[None, :]
    inner = int(np.log2(block // SPAN)) + 1
    return np.stack(
        [((level == l) & causal).astype(np.float32) for l in range(inner)]
    )


def state_kernel(head_count, k_ref, v_ref, o_ref):
    @pl.when(pl.program_id(0) == 0)
    def _():
        o_ref[...] = jnp.zeros_like(o_ref)

    dk = o_ref.shape[1]
    dv = o_ref.shape[2]
    for h in range(head_count):
        o_ref[h] += lax.dot_general(
            k_ref[:, h * dk:(h + 1) * dk], v_ref[:, h * dv:(h + 1) * dv],
            (((0,), (0,)), ((), ())), preferred_element_type=jnp.float32,
        )


def own_state(keys, values, head_count):
    rows, width = keys.shape
    dk = width // head_count
    dv = values.shape[1] // head_count
    tr = min(rows, 512)
    return pl.pallas_call(
        functools.partial(state_kernel, head_count),
        grid=(rows // tr,),
        in_specs=[
            pl.BlockSpec((tr, width), lambda r: (r, 0)),
            pl.BlockSpec((tr, values.shape[1]), lambda r: (r, 0)),
        ],
        out_specs=pl.BlockSpec((head_count, dk, dv), lambda r: (0, 0, 0)),
        out_shape=jax.ShapeDtypeStruct((head_count, dk, dv), jnp.float32),
        cost_estimate=pl.CostEstimate(
            flops=2 * rows * dk * dv * head_count,
            bytes_accessed=2 * rows * (dk + dv) * head_count + 4 * dk * dv * head_count,
            transcendentals=0,
        ),
        compiler_params=pltpu.CompilerParams(vmem_limit_bytes=64 * 1024 * 1024),
    )(keys, values)


def local_kernel(scale, rows, group, q_ref, k_ref, v_ref, m_ref, c_ref, *rest):
    o_ref = rest[-1]
    blocks = rows // TQ
    inner = c_ref.shape[0]
    dk = q_ref.shape[1] // group
    dv = v_ref.shape[1] // group
    for j in range(group):
        qc = slice(j * dk, (j + 1) * dk)
        vc = slice(j * dv, (j + 1) * dv)
        for a in range(blocks):
            r0 = a * TQ
            s = lax.dot_general(
                q_ref[r0:r0 + TQ, qc], k_ref[0:r0 + TQ, qc],
                (((1,), (1,)), ((), ())), preferred_element_type=jnp.float32,
            )
            s = s * scale
            mix = m_ref[j, r0:r0 + TQ, :]
            pieces = []
            for b in range(a):
                level = inner + (a ^ b).bit_length() - 1
                w = mix[:, level:level + 1]
                pieces.append((s[:, b * TQ:(b + 1) * TQ] * w).astype(jnp.bfloat16))
            wd = c_ref[0] * mix[:, 0:1]
            for l in range(1, inner):
                wd = wd + c_ref[l] * mix[:, l:l + 1]
            pieces.append((s[:, r0:r0 + TQ] * wd).astype(jnp.bfloat16))
            p = pieces[0] if len(pieces) == 1 else jnp.concatenate(pieces, axis=1)
            o_ref[r0:r0 + TQ, vc] = jnp.dot(
                p, v_ref[0:r0 + TQ, vc], preferred_element_type=jnp.float32
            )


def local_part(queries, keys, values, mix_t, masks, first, count, group, scale, prev):
    rows = queries.shape[0]
    head_count = mix_t.shape[0]
    dk = queries.shape[1] // head_count
    dv = values.shape[1] // head_count
    levels = mix_t.shape[2]
    blocks = rows // TQ
    tiles = blocks * (blocks + 1) // 2
    base = first // group
    in_specs = [
        pl.BlockSpec((rows, dk * group), lambda h: (0, h + base)),
        pl.BlockSpec((rows, dk * group), lambda h: (0, h + base)),
        pl.BlockSpec((rows, dv * group), lambda h: (0, h + base)),
        pl.BlockSpec((group, rows, levels), lambda h: (h + base, 0, 0)),
        pl.BlockSpec(masks.shape, lambda h: (0, 0, 0)),
    ]
    operands = [queries, keys, values, mix_t, masks]
    aliases = {}
    if prev is not None:
        in_specs.append(pl.BlockSpec(memory_space=pl.ANY))
        operands.append(prev)
        aliases = {5: 0}
    return pl.pallas_call(
        functools.partial(local_kernel, scale, rows, group),
        grid=(count // group,),
        in_specs=in_specs,
        out_specs=pl.BlockSpec((rows, dv * group), lambda h: (0, h + base)),
        out_shape=jax.ShapeDtypeStruct((rows, dv * head_count), jnp.float32),
        input_output_aliases=aliases,
        cost_estimate=pl.CostEstimate(
            flops=2 * tiles * TQ * TQ * (dk + dv) * count,
            bytes_accessed=(2 * rows * (2 * dk + dv) + 4 * rows * dv) * count,
            transcendentals=0,
        ),
        compiler_params=pltpu.CompilerParams(vmem_limit_bytes=64 * 1024 * 1024),
    )(*operands)


def cross_kernel(scale, rows, group, width, steps, q_ref, s_ref, m_ref, l_ref, o_ref):
    bits = s_ref.shape[0]
    dk = s_ref.shape[2]
    dv = s_ref.shape[3]

    def body(step):
        for j in range(group):
            c0 = (step * group + j) * width
            sib = jnp.concatenate([s_ref[b, j] for b in range(bits)], axis=1)
            for a in range(rows // TQ):
                r0 = a * TQ
                t = jnp.dot(
                    q_ref[r0:r0 + TQ, j * dk:(j + 1) * dk], sib,
                    preferred_element_type=jnp.float32,
                )
                w_all = m_ref[r0:r0 + TQ, c0:c0 + bits] * scale
                cross = w_all[:, 0:1] * t[:, 0:dv]
                for b in range(1, bits):
                    cross = cross + w_all[:, b:b + 1] * t[:, b * dv:(b + 1) * dv]
                o_ref[r0:r0 + TQ, j * dv:(j + 1) * dv] = (
                    l_ref[r0:r0 + TQ, j * dv:(j + 1) * dv] + cross
                )

    for step in range(steps):
        pl.when(pl.program_id(0) == step)(functools.partial(body, step))


def cross_all(queries, sibs, mix_c, local, scale, group, head_count, width):
    rows = queries.shape[0]
    dk = queries.shape[1] // head_count
    dv = sibs.shape[3]
    bits = sibs.shape[0]
    steps = head_count // group
    return pl.pallas_call(
        functools.partial(cross_kernel, scale, rows, group, width, steps),
        grid=(steps,),
        in_specs=[
            pl.BlockSpec((rows, dk * group), lambda g: (0, g)),
            pl.BlockSpec((bits, group, dk, dv), lambda g: (0, g, 0, 0)),
            pl.BlockSpec(mix_c.shape, lambda g: (0, 0)),
            pl.BlockSpec((rows, dv * group), lambda g: (0, g)),
        ],
        out_specs=pl.BlockSpec((rows, dv * group), lambda g: (0, g)),
        out_shape=jax.ShapeDtypeStruct((rows, dv * head_count), jnp.float32),
        input_output_aliases={3: 0},
        cost_estimate=pl.CostEstimate(
            flops=2 * rows * dk * dv * bits * head_count,
            bytes_accessed=(2 * rows * dk + 8 * rows * dv) * head_count,
            transcendentals=0,
        ),
        compiler_params=pltpu.CompilerParams(vmem_limit_bytes=64 * 1024 * 1024),
    )(queries, sibs, mix_c, local)


def swap(block, axis, bit, one_way=False):
    count = lax.axis_size(axis)
    route = []
    for low in range(count):
        high = low | 1 << bit
        if high != low and high < count:
            route.append((low, high))
            if not one_way:
                route.append((high, low))
    return lax.ppermute(block, axis, route)


def to_offset(block, axis, offset):
    count = lax.axis_size(axis)
    return lax.ppermute(block, axis, [(s, s ^ offset) for s in range(count)])


def shards(queries, keys, values, mixing):
    rows = queries.shape[0]
    head_count = mixing.shape[1]
    dk = queries.shape[1] // head_count
    scale = dk ** (-0.5)
    level_count = (rows // SPAN).bit_length()
    mix_t = mixing.transpose(1, 2, 0)
    masks = jnp.asarray(level_masks(TQ, level_count))

    state = own_state(keys, values, head_count)

    seq_count = lax.axis_size("seq")
    ctx_count = lax.axis_size("ctx")
    seq_bits = seq_count.bit_length() - 1
    ctx_bits = ctx_count.bit_length() - 1
    seq_place = lax.axis_index("seq")
    ctx_place = lax.axis_index("ctx")

    sibs = []
    flags = []
    running = state
    half = head_count // 2
    for bit in range(seq_bits):
        if bit == 0 or seq_count < 4:
            partner = swap(running, "seq", bit)
        else:
            mine = seq_place & 1
            sent = lax.dynamic_slice_in_dim(running, mine * half, half, 0)
            got = swap(sent, "seq", bit)
            other = swap(got, "seq", 0)
            lo = jnp.where(mine == 0, got, other)
            hi = jnp.where(mine == 0, other, got)
            partner = jnp.concatenate([lo, hi], axis=0)
        sibs.append(partner)
        flags.append(seq_place >> bit & 1)
        running = running + partner

    share = head_count // seq_count
    quarter = lax.dynamic_slice_in_dim(running, seq_place * share, share, 0)
    ctx_sibs = []
    for bit in range(ctx_bits):
        got = swap(quarter, "ctx", bit, one_way=(bit == ctx_bits - 1))
        ctx_sibs.append(got)
        if bit != ctx_bits - 1:
            quarter = quarter + got

    for bit in range(ctx_bits):
        part = lax.optimization_barrier(ctx_sibs[bit])
        parts = {0: part}
        for offset in range(1, seq_count):
            if offset & 1 and offset > 1:
                parts[offset] = to_offset(parts[offset ^ 1], "seq", 1)
            else:
                parts[offset] = to_offset(part, "seq", offset)
        full = []
        for owner in range(seq_count):
            pick = jnp.zeros_like(part)
            for offset in range(seq_count):
                pick = jnp.where((seq_place ^ offset) == owner, parts[offset], pick)
            full.append(pick)
        sibs.append(jnp.concatenate(full, axis=0))
        flags.append(ctx_place >> bit & 1)

    rounded = jnp.stack(
        [(flags[i].astype(jnp.float32) * sibs[i]).astype(jnp.bfloat16) for i in range(len(sibs))]
    )

    per = head_count // CHUNKS
    local = None
    for c in range(CHUNKS):
        local = local_part(
            queries, keys, values, mix_t, masks, c * per, per, LOCAL_GROUP, scale, local
        )
    bits = mixing.shape[0] - level_count
    width = 8 * -(-bits // 8)
    upper = jnp.pad(mixing[level_count:], ((0, width - bits), (0, 0), (0, 0)))
    mix_c = upper.transpose(2, 1, 0).reshape(rows, head_count * width)
    return cross_all(queries, rounded, mix_c, local, scale, CROSS_GROUP, head_count, width)


def solution(mesh):
    return jax.shard_map(
        shards,
        mesh=mesh,
        in_specs=(
            P(("ctx", "seq"), None),
            P(("ctx", "seq"), None),
            P(("ctx", "seq"), None),
            P(None, None, ("ctx", "seq")),
        ),
        out_specs=P(("ctx", "seq"), None),
        check_vma=False,
    )
```

```python
import functools

import numpy as np
import jax
import jax.numpy as jnp
from jax import lax
from jax.experimental import pallas as pl
from jax.experimental.pallas import tpu as pltpu
from jax.sharding import PartitionSpec as P

SPAN = 64
TQ = 256
CHUNKS = 4
LOCAL_GROUP = 2


def level_masks(block, level_count):
    pos = np.arange(block)
    span = pos // SPAN
    crossed = span[:, None] ^ span[None, :]
    level = np.zeros_like(crossed)
    for power_index in range(level_count - 1):
        level = level + (crossed >= 2**power_index)
    causal = pos[:, None] >= pos[None, :]
    inner = int(np.log2(block // SPAN)) + 1
    return np.stack(
        [((level == l) & causal).astype(np.float32) for l in range(inner)]
    )


def state_kernel(head_count, k_ref, v_ref, o_ref):
    @pl.when(pl.program_id(0) == 0)
    def _():
        o_ref[...] = jnp.zeros_like(o_ref)

    dk = o_ref.shape[1]
    dv = o_ref.shape[2]
    for h in range(head_count):
        o_ref[h] += lax.dot_general(
            k_ref[:, h * dk:(h + 1) * dk], v_ref[:, h * dv:(h + 1) * dv],
            (((0,), (0,)), ((), ())), preferred_element_type=jnp.float32,
        )


def own_state(keys, values, head_count):
    rows, width = keys.shape
    dk = width // head_count
    dv = values.shape[1] // head_count
    tr = min(rows, 512)
    return pl.pallas_call(
        functools.partial(state_kernel, head_count),
        grid=(rows // tr,),
        in_specs=[
            pl.BlockSpec((tr, width), lambda r: (r, 0)),
            pl.BlockSpec((tr, values.shape[1]), lambda r: (r, 0)),
        ],
        out_specs=pl.BlockSpec((head_count, dk, dv), lambda r: (0, 0, 0)),
        out_shape=jax.ShapeDtypeStruct((head_count, dk, dv), jnp.float32),
        cost_estimate=pl.CostEstimate(
            flops=2 * rows * dk * dv * head_count,
            bytes_accessed=2 * rows * (dk + dv) * head_count + 4 * dk * dv * head_count,
            transcendentals=0,
        ),
        compiler_params=pltpu.CompilerParams(vmem_limit_bytes=64 * 1024 * 1024),
    )(keys, values)


def local_kernel(scale, rows, group, q_ref, k_ref, v_ref, m_ref, c_ref, *rest):
    o_ref = rest[-1]
    blocks = rows // TQ
    inner = c_ref.shape[0]
    dk = q_ref.shape[1] // group
    dv = v_ref.shape[1] // group
    for j in range(group):
        qc = slice(j * dk, (j + 1) * dk)
        vc = slice(j * dv, (j + 1) * dv)
        for a in range(blocks):
            r0 = a * TQ
            s = lax.dot_general(
                q_ref[r0:r0 + TQ, qc], k_ref[0:r0 + TQ, qc],
                (((1,), (1,)), ((), ())), preferred_element_type=jnp.float32,
            )
            s = s * scale
            mix = m_ref[j, r0:r0 + TQ, :]
            pieces = []
            for b in range(a):
                level = inner + (a ^ b).bit_length() - 1
                w = mix[:, level:level + 1]
                pieces.append((s[:, b * TQ:(b + 1) * TQ] * w).astype(jnp.bfloat16))
            wd = c_ref[0] * mix[:, 0:1]
            for l in range(1, inner):
                wd = wd + c_ref[l] * mix[:, l:l + 1]
            pieces.append((s[:, r0:r0 + TQ] * wd).astype(jnp.bfloat16))
            p = pieces[0] if len(pieces) == 1 else jnp.concatenate(pieces, axis=1)
            o_ref[r0:r0 + TQ, vc] = jnp.dot(
                p, v_ref[0:r0 + TQ, vc], preferred_element_type=jnp.float32
            )


def local_part(queries, keys, values, mix_t, masks, first, count, group, scale, prev):
    rows = queries.shape[0]
    head_count = mix_t.shape[0]
    dk = queries.shape[1] // head_count
    dv = values.shape[1] // head_count
    levels = mix_t.shape[2]
    blocks = rows // TQ
    tiles = blocks * (blocks + 1) // 2
    base = first // group
    in_specs = [
        pl.BlockSpec((rows, dk * group), lambda h: (0, h + base)),
        pl.BlockSpec((rows, dk * group), lambda h: (0, h + base)),
        pl.BlockSpec((rows, dv * group), lambda h: (0, h + base)),
        pl.BlockSpec((group, rows, levels), lambda h: (h + base, 0, 0)),
        pl.BlockSpec(masks.shape, lambda h: (0, 0, 0)),
    ]
    operands = [queries, keys, values, mix_t, masks]
    aliases = {}
    if prev is not None:
        in_specs.append(pl.BlockSpec(memory_space=pl.ANY))
        operands.append(prev)
        aliases = {5: 0}
    return pl.pallas_call(
        functools.partial(local_kernel, scale, rows, group),
        grid=(count // group,),
        in_specs=in_specs,
        out_specs=pl.BlockSpec((rows, dv * group), lambda h: (0, h + base)),
        out_shape=jax.ShapeDtypeStruct((rows, dv * head_count), jnp.float32),
        input_output_aliases=aliases,
        cost_estimate=pl.CostEstimate(
            flops=2 * tiles * TQ * TQ * (dk + dv) * count,
            bytes_accessed=(2 * rows * (2 * dk + dv) + 4 * rows * dv) * count,
            transcendentals=0,
        ),
        compiler_params=pltpu.CompilerParams(vmem_limit_bytes=64 * 1024 * 1024),
    )(*operands)


def cross_kernel(scale, rows, first_level, group, n_seq, n_ctx, sp_ref, q_ref, m_ref, l_ref, *rest):
    o_ref = rest[-1]
    seq_refs = rest[:n_seq]
    ctx_refs = rest[n_seq:n_seq + n_ctx]
    bits = n_seq + n_ctx
    dk = q_ref.shape[1] // group
    dv = l_ref.shape[1] // group
    for j in range(group):
        blocks = [seq_refs[b][j] for b in range(n_seq)]
        blocks += [ctx_refs[c][0, j] for c in range(n_ctx)]
        sib = jnp.concatenate(
            [
                (sp_ref[1 + b].astype(jnp.float32) * blocks[b]).astype(jnp.bfloat16)
                for b in range(bits)
            ],
            axis=1,
        )
        for a in range(rows // TQ):
            r0 = a * TQ
            t = jnp.dot(
                q_ref[r0:r0 + TQ, j * dk:(j + 1) * dk], sib,
                preferred_element_type=jnp.float32,
            )
            w_all = m_ref[j, r0:r0 + TQ, first_level:first_level + bits] * scale
            cross = w_all[:, 0:1] * t[:, 0:dv]
            for b in range(1, bits):
                cross = cross + w_all[:, b:b + 1] * t[:, b * dv:(b + 1) * dv]
            o_ref[r0:r0 + TQ, j * dv:(j + 1) * dv] = (
                l_ref[r0:r0 + TQ, j * dv:(j + 1) * dv] + cross
            )


def cross_all(queries, scalars, seq_sibs, ctx_stacks, mix_t, local, scale, first_level, group):
    rows = queries.shape[0]
    head_count = mix_t.shape[0]
    dk = queries.shape[1] // head_count
    levels = mix_t.shape[2]
    dv = local.shape[1] // head_count
    n_seq = len(seq_sibs)
    n_ctx = len(ctx_stacks)
    bits = n_seq + n_ctx
    in_specs = [
        pl.BlockSpec((rows, dk * group), lambda g, sp: (0, g)),
        pl.BlockSpec((group, rows, levels), lambda g, sp: (g, 0, 0)),
        pl.BlockSpec((rows, dv * group), lambda g, sp: (0, g)),
    ]
    for x in seq_sibs:
        in_specs.append(pl.BlockSpec((group, dk, dv), lambda g, sp: (g, 0, 0)))
    for x in ctx_stacks:
        in_specs.append(
            pl.BlockSpec((1, group, dk, dv), lambda g, sp: (jnp.bitwise_xor(sp[0], g), 0, 0, 0))
        )
    return pl.pallas_call(
        functools.partial(cross_kernel, scale, rows, first_level, group, n_seq, n_ctx),
        grid_spec=pltpu.PrefetchScalarGridSpec(
            num_scalar_prefetch=1,
            grid=(head_count // group,),
            in_specs=in_specs,
            out_specs=pl.BlockSpec((rows, dv * group), lambda g, sp: (0, g)),
        ),
        out_shape=jax.ShapeDtypeStruct((rows, dv * head_count), jnp.float32),
        input_output_aliases={3: 0},
        cost_estimate=pl.CostEstimate(
            flops=2 * rows * dk * dv * bits * head_count,
            bytes_accessed=(2 * rows * dk + 8 * rows * dv) * head_count,
            transcendentals=0,
        ),
        compiler_params=pltpu.CompilerParams(vmem_limit_bytes=64 * 1024 * 1024),
    )(scalars, queries, mix_t, local, *seq_sibs, *ctx_stacks)


def swap(block, axis, bit, one_way=False):
    count = lax.axis_size(axis)
    route = []
    for low in range(count):
        high = low | 1 << bit
        if high != low and high < count:
            route.append((low, high))
            if not one_way:
                route.append((high, low))
    return lax.ppermute(block, axis, route)


def to_offset(block, axis, offset):
    count = lax.axis_size(axis)
    return lax.ppermute(block, axis, [(s, s ^ offset) for s in range(count)])


def shards(queries, keys, values, mixing):
    rows = queries.shape[0]
    head_count = mixing.shape[1]
    dk = queries.shape[1] // head_count
    scale = dk ** (-0.5)
    level_count = (rows // SPAN).bit_length()
    mix_t = mixing.transpose(1, 2, 0)
    masks = jnp.asarray(level_masks(TQ, level_count))

    state = own_state(keys, values, head_count)

    seq_count = lax.axis_size("seq")
    ctx_count = lax.axis_size("ctx")
    seq_bits = seq_count.bit_length() - 1
    ctx_bits = ctx_count.bit_length() - 1
    seq_place = lax.axis_index("seq")
    ctx_place = lax.axis_index("ctx")

    sibs = []
    flags = []
    running = state
    half = head_count // 2
    for bit in range(seq_bits):
        if bit == 0 or seq_count < 4:
            partner = swap(running, "seq", bit)
        else:
            mine = seq_place & 1
            sent = lax.dynamic_slice_in_dim(running, mine * half, half, 0)
            got = swap(sent, "seq", bit)
            other = swap(got, "seq", 0)
            lo = jnp.where(mine == 0, got, other)
            hi = jnp.where(mine == 0, other, got)
            partner = jnp.concatenate([lo, hi], axis=0)
        sibs.append(partner)
        flags.append(seq_place >> bit & 1)
        running = running + partner

    share = head_count // seq_count
    quarter = lax.dynamic_slice_in_dim(running, seq_place * share, share, 0)
    ctx_sibs = []
    for bit in range(ctx_bits):
        got = swap(quarter, "ctx", bit, one_way=(bit == ctx_bits - 1))
        ctx_sibs.append(got)
        if bit != ctx_bits - 1:
            quarter = quarter + got

    ctx_stacks = []
    for bit in range(ctx_bits):
        part = lax.optimization_barrier(ctx_sibs[bit])
        parts = {0: part}
        for offset in range(1, seq_count):
            if offset & 1 and offset > 1:
                parts[offset] = to_offset(parts[offset ^ 1], "seq", 1)
            else:
                parts[offset] = to_offset(part, "seq", offset)
        ctx_stacks.append(jnp.stack([parts[o] for o in range(seq_count)]))
        flags.append(ctx_place >> bit & 1)
    scalars = jnp.stack([seq_place] + flags).astype(jnp.int32)

    per = head_count // CHUNKS
    local = None
    for c in range(CHUNKS):
        local = local_part(
            queries, keys, values, mix_t, masks, c * per, per, LOCAL_GROUP, scale, local
        )
    return cross_all(
        queries, scalars, sibs, ctx_stacks, mix_t, local, scale, level_count,
        head_count // seq_count,
    )


def solution(mesh):
    return jax.shard_map(
        shards,
        mesh=mesh,
        in_specs=(
            P(("ctx", "seq"), None),
            P(("ctx", "seq"), None),
            P(("ctx", "seq"), None),
            P(None, None, ("ctx", "seq")),
        ),
        out_specs=P(("ctx", "seq"), None),
        check_vma=False,
    )
```

```python
import functools

import numpy as np
import jax
import jax.numpy as jnp
from jax import lax
from jax.experimental import pallas as pl
from jax.experimental.pallas import tpu as pltpu
from jax.sharding import PartitionSpec as P

SPAN = 64
TQ = 256
CHUNKS = 4
LOCAL_GROUP = 2


def level_masks(block, level_count):
    pos = np.arange(block)
    span = pos // SPAN
    crossed = span[:, None] ^ span[None, :]
    level = np.zeros_like(crossed)
    for power_index in range(level_count - 1):
        level = level + (crossed >= 2**power_index)
    causal = pos[:, None] >= pos[None, :]
    inner = int(np.log2(block // SPAN)) + 1
    return np.stack(
        [((level == l) & causal).astype(np.float32) for l in range(inner)]
    )


def state_kernel(head_count, k_ref, v_ref, o_ref):
    @pl.when(pl.program_id(0) == 0)
    def _():
        o_ref[...] = jnp.zeros_like(o_ref)

    dk = o_ref.shape[1]
    dv = o_ref.shape[2]
    for h in range(head_count):
        o_ref[h] += lax.dot_general(
            k_ref[:, h * dk:(h + 1) * dk], v_ref[:, h * dv:(h + 1) * dv],
            (((0,), (0,)), ((), ())), preferred_element_type=jnp.float32,
        )


def own_state(keys, values, head_count):
    rows, width = keys.shape
    dk = width // head_count
    dv = values.shape[1] // head_count
    tr = min(rows, 512)
    return pl.pallas_call(
        functools.partial(state_kernel, head_count),
        grid=(rows // tr,),
        in_specs=[
            pl.BlockSpec((tr, width), lambda r: (r, 0)),
            pl.BlockSpec((tr, values.shape[1]), lambda r: (r, 0)),
        ],
        out_specs=pl.BlockSpec((head_count, dk, dv), lambda r: (0, 0, 0)),
        out_shape=jax.ShapeDtypeStruct((head_count, dk, dv), jnp.float32),
        cost_estimate=pl.CostEstimate(
            flops=2 * rows * dk * dv * head_count,
            bytes_accessed=2 * rows * (dk + dv) * head_count + 4 * dk * dv * head_count,
            transcendentals=0,
        ),
        compiler_params=pltpu.CompilerParams(vmem_limit_bytes=64 * 1024 * 1024),
    )(keys, values)


def local_kernel(scale, rows, group, q_ref, k_ref, v_ref, m_ref, c_ref, *rest):
    o_ref = rest[-1]
    blocks = rows // TQ
    inner = c_ref.shape[0]
    dk = q_ref.shape[1] // group
    dv = v_ref.shape[1] // group
    for j in range(group):
        qc = slice(j * dk, (j + 1) * dk)
        vc = slice(j * dv, (j + 1) * dv)
        for a in range(blocks):
            r0 = a * TQ
            s = lax.dot_general(
                q_ref[r0:r0 + TQ, qc], k_ref[0:r0 + TQ, qc],
                (((1,), (1,)), ((), ())), preferred_element_type=jnp.float32,
            )
            s = s * scale
            mix = m_ref[j, r0:r0 + TQ, :]
            pieces = []
            for b in range(a):
                level = inner + (a ^ b).bit_length() - 1
                w = mix[:, level:level + 1]
                pieces.append((s[:, b * TQ:(b + 1) * TQ] * w).astype(jnp.bfloat16))
            wd = c_ref[0] * mix[:, 0:1]
            for l in range(1, inner):
                wd = wd + c_ref[l] * mix[:, l:l + 1]
            pieces.append((s[:, r0:r0 + TQ] * wd).astype(jnp.bfloat16))
            p = pieces[0] if len(pieces) == 1 else jnp.concatenate(pieces, axis=1)
            o_ref[r0:r0 + TQ, vc] = jnp.dot(
                p, v_ref[0:r0 + TQ, vc], preferred_element_type=jnp.float32
            )


def local_part(queries, keys, values, mix_t, masks, first, count, group, scale, prev):
    rows = queries.shape[0]
    head_count = mix_t.shape[0]
    dk = queries.shape[1] // head_count
    dv = values.shape[1] // head_count
    levels = mix_t.shape[2]
    blocks = rows // TQ
    tiles = blocks * (blocks + 1) // 2
    base = first // group
    in_specs = [
        pl.BlockSpec((rows, dk * group), lambda h: (0, h + base)),
        pl.BlockSpec((rows, dk * group), lambda h: (0, h + base)),
        pl.BlockSpec((rows, dv * group), lambda h: (0, h + base)),
        pl.BlockSpec((group, rows, levels), lambda h: (h + base, 0, 0)),
        pl.BlockSpec(masks.shape, lambda h: (0, 0, 0)),
    ]
    operands = [queries, keys, values, mix_t, masks]
    aliases = {}
    if prev is not None:
        in_specs.append(pl.BlockSpec(memory_space=pl.ANY))
        operands.append(prev)
        aliases = {5: 0}
    return pl.pallas_call(
        functools.partial(local_kernel, scale, rows, group),
        grid=(count // group,),
        in_specs=in_specs,
        out_specs=pl.BlockSpec((rows, dv * group), lambda h: (0, h + base)),
        out_shape=jax.ShapeDtypeStruct((rows, dv * head_count), jnp.float32),
        input_output_aliases=aliases,
        cost_estimate=pl.CostEstimate(
            flops=2 * tiles * TQ * TQ * (dk + dv) * count,
            bytes_accessed=(2 * rows * (2 * dk + dv) + 4 * rows * dv) * count,
            transcendentals=0,
        ),
        compiler_params=pltpu.CompilerParams(vmem_limit_bytes=64 * 1024 * 1024),
    )(*operands)


def cross_kernel(scale, rows, first_level, group, kinds, halves, sp_ref, q_ref, m_ref, l_ref, *rest):
    o_ref = rest[-1]
    n_seq = len(kinds)
    seq_refs = []
    at = 0
    for two in kinds:
        seq_refs.append((rest[at], rest[at + 1]) if two else rest[at])
        at += 2 if two else 1
    n_ctx = len(rest) - 1 - at
    ctx_refs = rest[at:at + n_ctx]
    bits = n_seq + n_ctx
    dk = q_ref.shape[1] // group
    dv = l_ref.shape[1] // group
    for j in range(group):
        blocks = []
        for b in range(n_seq):
            if isinstance(seq_refs[b], tuple):
                got_ref, other_ref = seq_refs[b]
                use_got = pl.program_id(0) // halves == jnp.bitwise_and(sp_ref[0], 1)
                blocks.append(jnp.where(use_got, got_ref[j], other_ref[j]))
            else:
                blocks.append(seq_refs[b][j])
        blocks += [ctx_refs[c][0, j] for c in range(n_ctx)]
        sib = jnp.concatenate(
            [
                (sp_ref[1 + b].astype(jnp.float32) * blocks[b]).astype(jnp.bfloat16)
                for b in range(bits)
            ],
            axis=1,
        )
        for a in range(rows // TQ):
            r0 = a * TQ
            t = jnp.dot(
                q_ref[r0:r0 + TQ, j * dk:(j + 1) * dk], sib,
                preferred_element_type=jnp.float32,
            )
            w_all = m_ref[j, r0:r0 + TQ, first_level:first_level + bits] * scale
            cross = w_all[:, 0:1] * t[:, 0:dv]
            for b in range(1, bits):
                cross = cross + w_all[:, b:b + 1] * t[:, b * dv:(b + 1) * dv]
            o_ref[r0:r0 + TQ, j * dv:(j + 1) * dv] = (
                l_ref[r0:r0 + TQ, j * dv:(j + 1) * dv] + cross
            )


def cross_all(queries, scalars, seq_sibs, ctx_stacks, mix_t, local, scale, first_level, group):
    rows = queries.shape[0]
    head_count = mix_t.shape[0]
    dk = queries.shape[1] // head_count
    levels = mix_t.shape[2]
    dv = local.shape[1] // head_count
    n_seq = len(seq_sibs)
    n_ctx = len(ctx_stacks)
    bits = n_seq + n_ctx
    in_specs = [
        pl.BlockSpec((rows, dk * group), lambda g, sp: (0, g)),
        pl.BlockSpec((group, rows, levels), lambda g, sp: (g, 0, 0)),
        pl.BlockSpec((rows, dv * group), lambda g, sp: (0, g)),
    ]
    kinds = []
    flat = []
    halves = head_count // 2 // group
    for x in seq_sibs:
        if isinstance(x, tuple):
            kinds.append(True)
            for y in x:
                in_specs.append(pl.BlockSpec((group, dk, dv), lambda g, sp: (g % halves, 0, 0)))
                flat.append(y)
        else:
            kinds.append(False)
            in_specs.append(pl.BlockSpec((group, dk, dv), lambda g, sp: (g, 0, 0)))
            flat.append(x)
    for x in ctx_stacks:
        in_specs.append(
            pl.BlockSpec((1, group, dk, dv), lambda g, sp: (jnp.bitwise_xor(sp[0], g), 0, 0, 0))
        )
    return pl.pallas_call(
        functools.partial(cross_kernel, scale, rows, first_level, group, tuple(kinds), halves),
        grid_spec=pltpu.PrefetchScalarGridSpec(
            num_scalar_prefetch=1,
            grid=(head_count // group,),
            in_specs=in_specs,
            out_specs=pl.BlockSpec((rows, dv * group), lambda g, sp: (0, g)),
        ),
        out_shape=jax.ShapeDtypeStruct((rows, dv * head_count), jnp.float32),
        input_output_aliases={3: 0},
        cost_estimate=pl.CostEstimate(
            flops=2 * rows * dk * dv * bits * head_count,
            bytes_accessed=(2 * rows * dk + 8 * rows * dv) * head_count,
            transcendentals=0,
        ),
        compiler_params=pltpu.CompilerParams(vmem_limit_bytes=64 * 1024 * 1024),
    )(scalars, queries, mix_t, local, *flat, *ctx_stacks)


def swap(block, axis, bit, one_way=False):
    count = lax.axis_size(axis)
    route = []
    for low in range(count):
        high = low | 1 << bit
        if high != low and high < count:
            route.append((low, high))
            if not one_way:
                route.append((high, low))
    return lax.ppermute(block, axis, route)


def to_offset(block, axis, offset):
    count = lax.axis_size(axis)
    return lax.ppermute(block, axis, [(s, s ^ offset) for s in range(count)])


def shards(queries, keys, values, mixing):
    rows = queries.shape[0]
    head_count = mixing.shape[1]
    dk = queries.shape[1] // head_count
    scale = dk ** (-0.5)
    level_count = (rows // SPAN).bit_length()
    mix_t = mixing.transpose(1, 2, 0)
    masks = jnp.asarray(level_masks(TQ, level_count))

    state = own_state(keys, values, head_count)

    seq_count = lax.axis_size("seq")
    ctx_count = lax.axis_size("ctx")
    seq_bits = seq_count.bit_length() - 1
    ctx_bits = ctx_count.bit_length() - 1
    seq_place = lax.axis_index("seq")
    ctx_place = lax.axis_index("ctx")

    sibs = []
    flags = []
    running = state
    half = head_count // 2
    for bit in range(seq_bits):
        if bit == 0 or seq_count < 4:
            partner = swap(running, "seq", bit)
            sibs.append(partner)
        else:
            mine = seq_place & 1
            sent = lax.dynamic_slice_in_dim(running, mine * half, half, 0)
            got = swap(sent, "seq", bit)
            other = swap(got, "seq", 0)
            lo = jnp.where(mine == 0, got, other)
            hi = jnp.where(mine == 0, other, got)
            partner = jnp.concatenate([lo, hi], axis=0)
            sibs.append((got, other))
        flags.append(seq_place >> bit & 1)
        running = running + partner

    share = head_count // seq_count
    quarter = lax.dynamic_slice_in_dim(running, seq_place * share, share, 0)
    ctx_sibs = []
    for bit in range(ctx_bits):
        got = swap(quarter, "ctx", bit, one_way=(bit == ctx_bits - 1))
        ctx_sibs.append(got)
        if bit != ctx_bits - 1:
            quarter = quarter + got

    ctx_stacks = []
    for bit in range(ctx_bits):
        part = lax.optimization_barrier(ctx_sibs[bit])
        parts = {0: part}
        for offset in range(1, seq_count):
            if offset & 1 and offset > 1:
                parts[offset] = to_offset(parts[offset ^ 1], "seq", 1)
            else:
                parts[offset] = to_offset(part, "seq", offset)
        ctx_stacks.append(jnp.stack([parts[o] for o in range(seq_count)]))
        flags.append(ctx_place >> bit & 1)
    scalars = jnp.stack([seq_place] + flags).astype(jnp.int32)

    per = head_count // CHUNKS
    local = None
    for c in range(CHUNKS):
        local = local_part(
            queries, keys, values, mix_t, masks, c * per, per, LOCAL_GROUP, scale, local
        )
    return cross_all(
        queries, scalars, sibs, ctx_stacks, mix_t, local, scale, level_count,
        head_count // seq_count,
    )


def solution(mesh):
    return jax.shard_map(
        shards,
        mesh=mesh,
        in_specs=(
            P(("ctx", "seq"), None),
            P(("ctx", "seq"), None),
            P(("ctx", "seq"), None),
            P(None, None, ("ctx", "seq")),
        ),
        out_specs=P(("ctx", "seq"), None),
        check_vma=False,
    )
```

```python
import functools

import numpy as np
import jax
import jax.numpy as jnp
from jax import lax
from jax.experimental import pallas as pl
from jax.experimental.pallas import tpu as pltpu
from jax.sharding import PartitionSpec as P

SPAN = 64
TQ = 256
CHUNKS = 4
LOCAL_GROUP = 2


def level_masks(block, level_count):
    pos = np.arange(block)
    span = pos // SPAN
    crossed = span[:, None] ^ span[None, :]
    level = np.zeros_like(crossed)
    for power_index in range(level_count - 1):
        level = level + (crossed >= 2**power_index)
    causal = pos[:, None] >= pos[None, :]
    inner = int(np.log2(block // SPAN)) + 1
    return np.stack(
        [((level == l) & causal).astype(np.float32) for l in range(inner)]
    )


def state_kernel(head_count, k_ref, v_ref, o_ref):
    @pl.when(pl.program_id(0) == 0)
    def _():
        o_ref[...] = jnp.zeros_like(o_ref)

    dk = o_ref.shape[1]
    dv = o_ref.shape[2]
    for h in range(head_count):
        o_ref[h] += lax.dot_general(
            k_ref[:, h * dk:(h + 1) * dk], v_ref[:, h * dv:(h + 1) * dv],
            (((0,), (0,)), ((), ())), preferred_element_type=jnp.float32,
        )


def own_state(keys, values, head_count):
    rows, width = keys.shape
    dk = width // head_count
    dv = values.shape[1] // head_count
    tr = min(rows, 512)
    return pl.pallas_call(
        functools.partial(state_kernel, head_count),
        grid=(rows // tr,),
        in_specs=[
            pl.BlockSpec((tr, width), lambda r: (r, 0)),
            pl.BlockSpec((tr, values.shape[1]), lambda r: (r, 0)),
        ],
        out_specs=pl.BlockSpec((head_count, dk, dv), lambda r: (0, 0, 0)),
        out_shape=jax.ShapeDtypeStruct((head_count, dk, dv), jnp.float32),
        cost_estimate=pl.CostEstimate(
            flops=2 * rows * dk * dv * head_count,
            bytes_accessed=2 * rows * (dk + dv) * head_count + 4 * dk * dv * head_count,
            transcendentals=0,
        ),
        compiler_params=pltpu.CompilerParams(vmem_limit_bytes=64 * 1024 * 1024),
    )(keys, values)


def local_kernel(scale, rows, group, q_ref, k_ref, v_ref, m_ref, c_ref, *rest):
    o_ref = rest[-1]
    blocks = rows // TQ
    inner = c_ref.shape[0]
    dk = q_ref.shape[1] // group
    dv = v_ref.shape[1] // group
    for j in range(group):
        qc = slice(j * dk, (j + 1) * dk)
        vc = slice(j * dv, (j + 1) * dv)
        for a in range(blocks):
            r0 = a * TQ
            s = lax.dot_general(
                q_ref[r0:r0 + TQ, qc], k_ref[0:r0 + TQ, qc],
                (((1,), (1,)), ((), ())), preferred_element_type=jnp.float32,
            )
            s = s * scale
            mix = m_ref[j, r0:r0 + TQ, :]
            pieces = []
            for b in range(a):
                level = inner + (a ^ b).bit_length() - 1
                w = mix[:, level:level + 1]
                pieces.append((s[:, b * TQ:(b + 1) * TQ] * w).astype(jnp.bfloat16))
            wd = c_ref[0] * mix[:, 0:1]
            for l in range(1, inner):
                wd = wd + c_ref[l] * mix[:, l:l + 1]
            pieces.append((s[:, r0:r0 + TQ] * wd).astype(jnp.bfloat16))
            p = pieces[0] if len(pieces) == 1 else jnp.concatenate(pieces, axis=1)
            o_ref[r0:r0 + TQ, vc] = jnp.dot(
                p, v_ref[0:r0 + TQ, vc], preferred_element_type=jnp.float32
            )


def local_part(queries, keys, values, mix_t, masks, first, count, group, scale, prev):
    rows = queries.shape[0]
    head_count = mix_t.shape[0]
    dk = queries.shape[1] // head_count
    dv = values.shape[1] // head_count
    levels = mix_t.shape[2]
    blocks = rows // TQ
    tiles = blocks * (blocks + 1) // 2
    base = first // group
    in_specs = [
        pl.BlockSpec((rows, dk * group), lambda h: (0, h + base)),
        pl.BlockSpec((rows, dk * group), lambda h: (0, h + base)),
        pl.BlockSpec((rows, dv * group), lambda h: (0, h + base)),
        pl.BlockSpec((group, rows, levels), lambda h: (h + base, 0, 0)),
        pl.BlockSpec(masks.shape, lambda h: (0, 0, 0)),
    ]
    operands = [queries, keys, values, mix_t, masks]
    aliases = {}
    if prev is not None:
        in_specs.append(pl.BlockSpec(memory_space=pl.ANY))
        operands.append(prev)
        aliases = {5: 0}
    return pl.pallas_call(
        functools.partial(local_kernel, scale, rows, group),
        grid=(count // group,),
        in_specs=in_specs,
        out_specs=pl.BlockSpec((rows, dv * group), lambda h: (0, h + base)),
        out_shape=jax.ShapeDtypeStruct((rows, dv * head_count), jnp.float32),
        input_output_aliases=aliases,
        cost_estimate=pl.CostEstimate(
            flops=2 * tiles * TQ * TQ * (dk + dv) * count,
            bytes_accessed=(2 * rows * (2 * dk + dv) + 4 * rows * dv) * count,
            transcendentals=0,
        ),
        compiler_params=pltpu.CompilerParams(vmem_limit_bytes=64 * 1024 * 1024),
    )(*operands)


def cross_kernel(scale, rows, first_level, group, n_seq, n_ctx, sp_ref, q_ref, m_ref, l_ref, *rest):
    o_ref = rest[-1]
    seq_refs = rest[:n_seq]
    ctx_refs = rest[n_seq:n_seq + n_ctx]
    bits = n_seq + n_ctx
    dk = q_ref.shape[1] // group
    dv = l_ref.shape[1] // group
    for j in range(group):
        blocks = [seq_refs[b][j] for b in range(n_seq)]
        blocks += [ctx_refs[c][0, j] for c in range(n_ctx)]
        sib = jnp.concatenate(
            [
                (sp_ref[1 + b].astype(jnp.float32) * blocks[b]).astype(jnp.bfloat16)
                for b in range(bits)
            ],
            axis=1,
        )
        for a in range(rows // TQ):
            r0 = a * TQ
            t = jnp.dot(
                q_ref[r0:r0 + TQ, j * dk:(j + 1) * dk], sib,
                preferred_element_type=jnp.float32,
            )
            w_all = m_ref[j, r0:r0 + TQ, first_level:first_level + bits] * scale
            cross = w_all[:, 0:1] * t[:, 0:dv]
            for b in range(1, bits):
                cross = cross + w_all[:, b:b + 1] * t[:, b * dv:(b + 1) * dv]
            o_ref[r0:r0 + TQ, j * dv:(j + 1) * dv] = (
                l_ref[r0:r0 + TQ, j * dv:(j + 1) * dv] + cross
            )


def cross_all(queries, scalars, seq_sibs, ctx_stacks, mix_t, local, scale, first_level, group):
    rows = queries.shape[0]
    head_count = mix_t.shape[0]
    dk = queries.shape[1] // head_count
    levels = mix_t.shape[2]
    dv = local.shape[1] // head_count
    n_seq = len(seq_sibs)
    n_ctx = len(ctx_stacks)
    bits = n_seq + n_ctx
    in_specs = [
        pl.BlockSpec((rows, dk * group), lambda g, sp: (0, g)),
        pl.BlockSpec((group, rows, levels), lambda g, sp: (g, 0, 0)),
        pl.BlockSpec((rows, dv * group), lambda g, sp: (0, g)),
    ]
    for x in seq_sibs:
        in_specs.append(pl.BlockSpec((group, dk, dv), lambda g, sp: (g, 0, 0)))
    for x in ctx_stacks:
        in_specs.append(
            pl.BlockSpec((1, group, dk, dv), lambda g, sp: (jnp.bitwise_xor(sp[0], g), 0, 0, 0))
        )
    return pl.pallas_call(
        functools.partial(cross_kernel, scale, rows, first_level, group, n_seq, n_ctx),
        grid_spec=pltpu.PrefetchScalarGridSpec(
            num_scalar_prefetch=1,
            grid=(head_count // group,),
            in_specs=in_specs,
            out_specs=pl.BlockSpec((rows, dv * group), lambda g, sp: (0, g)),
        ),
        out_shape=jax.ShapeDtypeStruct((rows, dv * head_count), jnp.float32),
        input_output_aliases={3: 0},
        cost_estimate=pl.CostEstimate(
            flops=2 * rows * dk * dv * bits * head_count,
            bytes_accessed=(2 * rows * dk + 8 * rows * dv) * head_count,
            transcendentals=0,
        ),
        compiler_params=pltpu.CompilerParams(vmem_limit_bytes=64 * 1024 * 1024),
    )(scalars, queries, mix_t, local, *seq_sibs, *ctx_stacks)


def swap(block, axis, bit, one_way=False):
    count = lax.axis_size(axis)
    route = []
    for low in range(count):
        high = low | 1 << bit
        if high != low and high < count:
            route.append((low, high))
            if not one_way:
                route.append((high, low))
    return lax.ppermute(block, axis, route)


def to_offset(block, axis, offset):
    count = lax.axis_size(axis)
    return lax.ppermute(block, axis, [(s, s ^ offset) for s in range(count)])


def shards(queries, keys, values, mixing):
    rows = queries.shape[0]
    head_count = mixing.shape[1]
    dk = queries.shape[1] // head_count
    scale = dk ** (-0.5)
    level_count = (rows // SPAN).bit_length()
    mix_t = mixing.transpose(1, 2, 0)
    masks = jnp.asarray(level_masks(TQ, level_count))

    state = own_state(keys, values, head_count)

    seq_count = lax.axis_size("seq")
    ctx_count = lax.axis_size("ctx")
    seq_bits = seq_count.bit_length() - 1
    ctx_bits = ctx_count.bit_length() - 1
    seq_place = lax.axis_index("seq")
    ctx_place = lax.axis_index("ctx")

    sibs = []
    flags = []
    running = state
    half = head_count // 2
    for bit in range(seq_bits):
        if bit == 0 or seq_count < 4:
            partner = swap(running, "seq", bit)
        else:
            mine = seq_place & 1
            if bit == 1:
                sent = lax.dynamic_slice_in_dim(
                    lax.optimization_barrier(state), mine * half, half, 0
                ) + lax.dynamic_slice_in_dim(sibs[0], mine * half, half, 0)
            else:
                sent = lax.dynamic_slice_in_dim(running, mine * half, half, 0)
            got = swap(sent, "seq", bit)
            other = swap(got, "seq", 0)
            lo = jnp.where(mine == 0, got, other)
            hi = jnp.where(mine == 0, other, got)
            partner = jnp.concatenate([lo, hi], axis=0)
        sibs.append(partner)
        flags.append(seq_place >> bit & 1)
        running = running + partner

    share = head_count // seq_count
    quarter = lax.dynamic_slice_in_dim(running, seq_place * share, share, 0)
    ctx_sibs = []
    for bit in range(ctx_bits):
        got = swap(quarter, "ctx", bit, one_way=(bit == ctx_bits - 1))
        ctx_sibs.append(got)
        if bit != ctx_bits - 1:
            quarter = quarter + got

    ctx_stacks = []
    for bit in range(ctx_bits):
        part = lax.optimization_barrier(ctx_sibs[bit])
        parts = {0: part}
        for offset in range(1, seq_count):
            if offset & 1 and offset > 1:
                parts[offset] = to_offset(parts[offset ^ 1], "seq", 1)
            else:
                parts[offset] = to_offset(part, "seq", offset)
        ctx_stacks.append(jnp.stack([parts[o] for o in range(seq_count)]))
        flags.append(ctx_place >> bit & 1)
    scalars = jnp.stack([seq_place] + flags).astype(jnp.int32)

    per = head_count // CHUNKS
    local = None
    for c in range(CHUNKS):
        local = local_part(
            queries, keys, values, mix_t, masks, c * per, per, LOCAL_GROUP, scale, local
        )
    return cross_all(
        queries, scalars, sibs, ctx_stacks, mix_t, local, scale, level_count,
        head_count // seq_count,
    )


def solution(mesh):
    return jax.shard_map(
        shards,
        mesh=mesh,
        in_specs=(
            P(("ctx", "seq"), None),
            P(("ctx", "seq"), None),
            P(("ctx", "seq"), None),
            P(None, None, ("ctx", "seq")),
        ),
        out_specs=P(("ctx", "seq"), None),
        check_vma=False,
    )
```

```python
import functools

import numpy as np
import jax
import jax.numpy as jnp
from jax import lax
from jax.experimental import pallas as pl
from jax.experimental.pallas import tpu as pltpu
from jax.sharding import PartitionSpec as P

SPAN = 64
TQ = 256
CHUNKS = 4
LOCAL_GROUP = 2


def level_masks(block, level_count):
    pos = np.arange(block)
    span = pos // SPAN
    crossed = span[:, None] ^ span[None, :]
    level = np.zeros_like(crossed)
    for power_index in range(level_count - 1):
        level = level + (crossed >= 2**power_index)
    causal = pos[:, None] >= pos[None, :]
    inner = int(np.log2(block // SPAN)) + 1
    return np.stack(
        [((level == l) & causal).astype(np.float32) for l in range(inner)]
    )


def state_kernel(head_count, k_ref, v_ref, o_ref):
    @pl.when(pl.program_id(0) == 0)
    def _():
        o_ref[...] = jnp.zeros_like(o_ref)

    dk = o_ref.shape[1]
    dv = o_ref.shape[2]
    for h in range(head_count):
        o_ref[h] += lax.dot_general(
            k_ref[:, h * dk:(h + 1) * dk], v_ref[:, h * dv:(h + 1) * dv],
            (((0,), (0,)), ((), ())), preferred_element_type=jnp.float32,
        )


def own_state(keys, values, head_count):
    rows, width = keys.shape
    dk = width // head_count
    dv = values.shape[1] // head_count
    tr = min(rows, 512)
    return pl.pallas_call(
        functools.partial(state_kernel, head_count),
        grid=(rows // tr,),
        in_specs=[
            pl.BlockSpec((tr, width), lambda r: (r, 0)),
            pl.BlockSpec((tr, values.shape[1]), lambda r: (r, 0)),
        ],
        out_specs=pl.BlockSpec((head_count, dk, dv), lambda r: (0, 0, 0)),
        out_shape=jax.ShapeDtypeStruct((head_count, dk, dv), jnp.float32),
        cost_estimate=pl.CostEstimate(
            flops=2 * rows * dk * dv * head_count,
            bytes_accessed=2 * rows * (dk + dv) * head_count + 4 * dk * dv * head_count,
            transcendentals=0,
        ),
        compiler_params=pltpu.CompilerParams(vmem_limit_bytes=64 * 1024 * 1024),
    )(keys, values)


def local_kernel(scale, rows, group, q_ref, k_ref, v_ref, m_ref, c_ref, *rest):
    o_ref = rest[-1]
    blocks = rows // TQ
    inner = c_ref.shape[0]
    dk = q_ref.shape[1] // group
    dv = v_ref.shape[1] // group
    for j in range(group):
        qc = slice(j * dk, (j + 1) * dk)
        vc = slice(j * dv, (j + 1) * dv)
        for a in range(blocks):
            r0 = a * TQ
            s = lax.dot_general(
                q_ref[r0:r0 + TQ, qc], k_ref[0:r0 + TQ, qc],
                (((1,), (1,)), ((), ())), preferred_element_type=jnp.float32,
            )
            s = s * scale
            mix = m_ref[j, r0:r0 + TQ, :]
            pieces = []
            for b in range(a):
                level = inner + (a ^ b).bit_length() - 1
                w = mix[:, level:level + 1]
                pieces.append((s[:, b * TQ:(b + 1) * TQ] * w).astype(jnp.bfloat16))
            wd = c_ref[0] * mix[:, 0:1]
            for l in range(1, inner):
                wd = wd + c_ref[l] * mix[:, l:l + 1]
            pieces.append((s[:, r0:r0 + TQ] * wd).astype(jnp.bfloat16))
            p = pieces[0] if len(pieces) == 1 else jnp.concatenate(pieces, axis=1)
            o_ref[r0:r0 + TQ, vc] = jnp.dot(
                p, v_ref[0:r0 + TQ, vc], preferred_element_type=jnp.float32
            )


def local_part(queries, keys, values, mix_t, masks, first, count, group, scale, prev):
    rows = queries.shape[0]
    head_count = mix_t.shape[0]
    dk = queries.shape[1] // head_count
    dv = values.shape[1] // head_count
    levels = mix_t.shape[2]
    blocks = rows // TQ
    tiles = blocks * (blocks + 1) // 2
    base = first // group
    in_specs = [
        pl.BlockSpec((rows, dk * group), lambda h: (0, h + base)),
        pl.BlockSpec((rows, dk * group), lambda h: (0, h + base)),
        pl.BlockSpec((rows, dv * group), lambda h: (0, h + base)),
        pl.BlockSpec((group, rows, levels), lambda h: (h + base, 0, 0)),
        pl.BlockSpec(masks.shape, lambda h: (0, 0, 0)),
    ]
    operands = [queries, keys, values, mix_t, masks]
    aliases = {}
    if prev is not None:
        in_specs.append(pl.BlockSpec(memory_space=pl.ANY))
        operands.append(prev)
        aliases = {5: 0}
    return pl.pallas_call(
        functools.partial(local_kernel, scale, rows, group),
        grid=(count // group,),
        in_specs=in_specs,
        out_specs=pl.BlockSpec((rows, dv * group), lambda h: (0, h + base)),
        out_shape=jax.ShapeDtypeStruct((rows, dv * head_count), jnp.float32),
        input_output_aliases=aliases,
        cost_estimate=pl.CostEstimate(
            flops=2 * tiles * TQ * TQ * (dk + dv) * count,
            bytes_accessed=(2 * rows * (2 * dk + dv) + 4 * rows * dv) * count,
            transcendentals=0,
        ),
        compiler_params=pltpu.CompilerParams(vmem_limit_bytes=64 * 1024 * 1024),
    )(*operands)


def cross_kernel(scale, rows, first_level, group, n_seq, n_ctx, sp_ref, q_ref, m_ref, l_ref, *rest):
    o_ref = rest[-1]
    seq_refs = rest[:n_seq]
    ctx_refs = rest[n_seq:n_seq + n_ctx]
    bits = n_seq + n_ctx
    dk = q_ref.shape[1] // group
    dv = l_ref.shape[1] // group
    for j in range(group):
        blocks = [seq_refs[b][j] for b in range(n_seq)]
        blocks += [ctx_refs[c][0, j] for c in range(n_ctx)]
        sib = jnp.concatenate(
            [
                (sp_ref[1 + b].astype(jnp.float32) * blocks[b]).astype(jnp.bfloat16)
                for b in range(bits)
            ],
            axis=1,
        )
        for a in range(rows // TQ):
            r0 = a * TQ
            t = jnp.dot(
                q_ref[r0:r0 + TQ, j * dk:(j + 1) * dk], sib,
                preferred_element_type=jnp.float32,
            )
            w_all = m_ref[j, r0:r0 + TQ, first_level:first_level + bits] * scale
            cross = w_all[:, 0:1] * t[:, 0:dv]
            for b in range(1, bits):
                cross = cross + w_all[:, b:b + 1] * t[:, b * dv:(b + 1) * dv]
            o_ref[r0:r0 + TQ, j * dv:(j + 1) * dv] = (
                l_ref[r0:r0 + TQ, j * dv:(j + 1) * dv] + cross
            )


def cross_all(queries, scalars, seq_sibs, ctx_stacks, mix_t, local, scale, first_level, group):
    rows = queries.shape[0]
    head_count = mix_t.shape[0]
    dk = queries.shape[1] // head_count
    levels = mix_t.shape[2]
    dv = local.shape[1] // head_count
    n_seq = len(seq_sibs)
    n_ctx = len(ctx_stacks)
    bits = n_seq + n_ctx
    in_specs = [
        pl.BlockSpec((rows, dk * group), lambda g, sp: (0, g)),
        pl.BlockSpec((group, rows, levels), lambda g, sp: (g, 0, 0)),
        pl.BlockSpec((rows, dv * group), lambda g, sp: (0, g)),
    ]
    for x in seq_sibs:
        in_specs.append(pl.BlockSpec((group, dk, dv), lambda g, sp: (g, 0, 0)))
    for x in ctx_stacks:
        in_specs.append(
            pl.BlockSpec((1, group, dk, dv), lambda g, sp: (jnp.bitwise_xor(sp[0], g), 0, 0, 0))
        )
    return pl.pallas_call(
        functools.partial(cross_kernel, scale, rows, first_level, group, n_seq, n_ctx),
        grid_spec=pltpu.PrefetchScalarGridSpec(
            num_scalar_prefetch=1,
            grid=(head_count // group,),
            in_specs=in_specs,
            out_specs=pl.BlockSpec((rows, dv * group), lambda g, sp: (0, g)),
        ),
        out_shape=jax.ShapeDtypeStruct((rows, dv * head_count), jnp.float32),
        input_output_aliases={3: 0},
        cost_estimate=pl.CostEstimate(
            flops=2 * rows * dk * dv * bits * head_count,
            bytes_accessed=(2 * rows * dk + 8 * rows * dv) * head_count,
            transcendentals=0,
        ),
        compiler_params=pltpu.CompilerParams(vmem_limit_bytes=64 * 1024 * 1024),
    )(scalars, queries, mix_t, local, *seq_sibs, *ctx_stacks)


def swap(block, axis, bit, one_way=False):
    count = lax.axis_size(axis)
    route = []
    for low in range(count):
        high = low | 1 << bit
        if high != low and high < count:
            route.append((low, high))
            if not one_way:
                route.append((high, low))
    return lax.ppermute(block, axis, route)


def to_offset(block, axis, offset):
    count = lax.axis_size(axis)
    return lax.ppermute(block, axis, [(s, s ^ offset) for s in range(count)])


def shards(queries, keys, values, mixing):
    rows = queries.shape[0]
    head_count = mixing.shape[1]
    dk = queries.shape[1] // head_count
    scale = dk ** (-0.5)
    level_count = (rows // SPAN).bit_length()
    mix_t = mixing.transpose(1, 2, 0)
    masks = jnp.asarray(level_masks(TQ, level_count))

    state = own_state(keys, values, head_count)

    seq_count = lax.axis_size("seq")
    ctx_count = lax.axis_size("ctx")
    seq_bits = seq_count.bit_length() - 1
    ctx_bits = ctx_count.bit_length() - 1
    seq_place = lax.axis_index("seq")
    ctx_place = lax.axis_index("ctx")

    sibs = []
    flags = []
    running = state
    half = head_count // 2
    for bit in range(seq_bits):
        if bit == 0 or seq_count < 4:
            partner = swap(running, "seq", bit)
        else:
            mine = seq_place & 1
            if bit == 1:
                sent = lax.dynamic_slice_in_dim(
                    lax.optimization_barrier(state), mine * half, half, 0
                ) + lax.dynamic_slice_in_dim(sibs[0], mine * half, half, 0)
            else:
                sent = lax.dynamic_slice_in_dim(running, mine * half, half, 0)
            got = swap(sent, "seq", bit)
            other = swap(got, "seq", 0)
            lo = jnp.where(mine == 0, got, other)
            hi = jnp.where(mine == 0, other, got)
            partner = jnp.concatenate([lo, hi], axis=0)
        sibs.append(partner)
        flags.append(seq_place >> bit & 1)
        running = running + partner

    share = head_count // seq_count
    if seq_bits == 2:
        start = seq_place * share
        inner_at = start % half
        from_got = (seq_place >> 1) == (seq_place & 1)
        upper = jnp.where(
            from_got,
            lax.dynamic_slice_in_dim(got, inner_at, share, 0),
            lax.dynamic_slice_in_dim(other, inner_at, share, 0),
        )
        quarter = (
            lax.dynamic_slice_in_dim(lax.optimization_barrier(state), start, share, 0)
            + lax.dynamic_slice_in_dim(sibs[0], start, share, 0)
        ) + upper
    else:
        quarter = lax.dynamic_slice_in_dim(running, seq_place * share, share, 0)
    ctx_sibs = []
    for bit in range(ctx_bits):
        got = swap(quarter, "ctx", bit, one_way=(bit == ctx_bits - 1))
        ctx_sibs.append(got)
        if bit != ctx_bits - 1:
            quarter = quarter + got

    ctx_stacks = []
    for bit in range(ctx_bits):
        part = lax.optimization_barrier(ctx_sibs[bit])
        parts = {0: part}
        for offset in range(1, seq_count):
            if offset & 1 and offset > 1:
                parts[offset] = to_offset(parts[offset ^ 1], "seq", 1)
            else:
                parts[offset] = to_offset(part, "seq", offset)
        ctx_stacks.append(jnp.stack([parts[o] for o in range(seq_count)]))
        flags.append(ctx_place >> bit & 1)
    scalars = jnp.stack([seq_place] + flags).astype(jnp.int32)

    per = head_count // CHUNKS
    local = None
    for c in range(CHUNKS):
        local = local_part(
            queries, keys, values, mix_t, masks, c * per, per, LOCAL_GROUP, scale, local
        )
    return cross_all(
        queries, scalars, sibs, ctx_stacks, mix_t, local, scale, level_count,
        head_count // seq_count,
    )


def solution(mesh):
    return jax.shard_map(
        shards,
        mesh=mesh,
        in_specs=(
            P(("ctx", "seq"), None),
            P(("ctx", "seq"), None),
            P(("ctx", "seq"), None),
            P(None, None, ("ctx", "seq")),
        ),
        out_specs=P(("ctx", "seq"), None),
        check_vma=False,
    )
```

```python
import functools

import numpy as np
import jax
import jax.numpy as jnp
from jax import lax
from jax.experimental import pallas as pl
from jax.experimental.pallas import tpu as pltpu
from jax.sharding import PartitionSpec as P

SPAN = 64
TQ = 256
CHUNKS = 4
LOCAL_GROUP = 2


def level_masks(block, level_count):
    pos = np.arange(block)
    span = pos // SPAN
    crossed = span[:, None] ^ span[None, :]
    level = np.zeros_like(crossed)
    for power_index in range(level_count - 1):
        level = level + (crossed >= 2**power_index)
    causal = pos[:, None] >= pos[None, :]
    inner = int(np.log2(block // SPAN)) + 1
    return np.stack(
        [((level == l) & causal).astype(np.float32) for l in range(inner)]
    )


def state_kernel(head_count, k_ref, v_ref, o_ref):
    @pl.when(pl.program_id(0) == 0)
    def _():
        o_ref[...] = jnp.zeros_like(o_ref)

    dk = o_ref.shape[1]
    dv = o_ref.shape[2]
    for h in range(head_count):
        o_ref[h] += lax.dot_general(
            k_ref[:, h * dk:(h + 1) * dk], v_ref[:, h * dv:(h + 1) * dv],
            (((0,), (0,)), ((), ())), preferred_element_type=jnp.float32,
        )


def own_state(keys, values, head_count):
    rows, width = keys.shape
    dk = width // head_count
    dv = values.shape[1] // head_count
    tr = min(rows, 512)
    return pl.pallas_call(
        functools.partial(state_kernel, head_count),
        grid=(rows // tr,),
        in_specs=[
            pl.BlockSpec((tr, width), lambda r: (r, 0)),
            pl.BlockSpec((tr, values.shape[1]), lambda r: (r, 0)),
        ],
        out_specs=pl.BlockSpec((head_count, dk, dv), lambda r: (0, 0, 0)),
        out_shape=jax.ShapeDtypeStruct((head_count, dk, dv), jnp.float32),
        cost_estimate=pl.CostEstimate(
            flops=2 * rows * dk * dv * head_count,
            bytes_accessed=2 * rows * (dk + dv) * head_count + 4 * dk * dv * head_count,
            transcendentals=0,
        ),
        compiler_params=pltpu.CompilerParams(vmem_limit_bytes=64 * 1024 * 1024),
    )(keys, values)


def local_kernel(scale, rows, group, q_ref, k_ref, v_ref, m_ref, c_ref, *rest):
    o_ref = rest[-1]
    blocks = rows // TQ
    inner = c_ref.shape[0]
    dk = q_ref.shape[1] // group
    dv = v_ref.shape[1] // group
    for j in range(group):
        qc = slice(j * dk, (j + 1) * dk)
        vc = slice(j * dv, (j + 1) * dv)
        for a in range(blocks):
            r0 = a * TQ
            s = lax.dot_general(
                q_ref[r0:r0 + TQ, qc], k_ref[0:r0 + TQ, qc],
                (((1,), (1,)), ((), ())), preferred_element_type=jnp.float32,
            )
            s = s * scale
            mix = m_ref[j, r0:r0 + TQ, :]
            pieces = []
            for b in range(a):
                level = inner + (a ^ b).bit_length() - 1
                w = mix[:, level:level + 1]
                pieces.append((s[:, b * TQ:(b + 1) * TQ] * w).astype(jnp.bfloat16))
            wd = c_ref[0] * mix[:, 0:1]
            for l in range(1, inner):
                wd = wd + c_ref[l] * mix[:, l:l + 1]
            pieces.append((s[:, r0:r0 + TQ] * wd).astype(jnp.bfloat16))
            p = pieces[0] if len(pieces) == 1 else jnp.concatenate(pieces, axis=1)
            o_ref[r0:r0 + TQ, vc] = jnp.dot(
                p, v_ref[0:r0 + TQ, vc], preferred_element_type=jnp.float32
            )


def local_part(queries, keys, values, mix_t, masks, first, count, group, scale, prev):
    rows = queries.shape[0]
    head_count = mix_t.shape[0]
    dk = queries.shape[1] // head_count
    dv = values.shape[1] // head_count
    levels = mix_t.shape[2]
    blocks = rows // TQ
    tiles = blocks * (blocks + 1) // 2
    base = first // group
    in_specs = [
        pl.BlockSpec((rows, dk * group), lambda h: (0, h + base)),
        pl.BlockSpec((rows, dk * group), lambda h: (0, h + base)),
        pl.BlockSpec((rows, dv * group), lambda h: (0, h + base)),
        pl.BlockSpec((group, rows, levels), lambda h: (h + base, 0, 0)),
        pl.BlockSpec(masks.shape, lambda h: (0, 0, 0)),
    ]
    operands = [queries, keys, values, mix_t, masks]
    aliases = {}
    if prev is not None:
        in_specs.append(pl.BlockSpec(memory_space=pl.ANY))
        operands.append(prev)
        aliases = {5: 0}
    return pl.pallas_call(
        functools.partial(local_kernel, scale, rows, group),
        grid=(count // group,),
        in_specs=in_specs,
        out_specs=pl.BlockSpec((rows, dv * group), lambda h: (0, h + base)),
        out_shape=jax.ShapeDtypeStruct((rows, dv * head_count), jnp.float32),
        input_output_aliases=aliases,
        cost_estimate=pl.CostEstimate(
            flops=2 * tiles * TQ * TQ * (dk + dv) * count,
            bytes_accessed=(2 * rows * (2 * dk + dv) + 4 * rows * dv) * count,
            transcendentals=0,
        ),
        compiler_params=pltpu.CompilerParams(vmem_limit_bytes=64 * 1024 * 1024),
    )(*operands)


def cross_kernel(scale, rows, first_level, group, n_seq, n_ctx, sp_ref, q_ref, m_ref, l_ref, *rest):
    o_ref = rest[-1]
    seq_refs = rest[:n_seq]
    ctx_refs = rest[n_seq:n_seq + n_ctx]
    bits = n_seq + n_ctx
    dk = q_ref.shape[1] // group
    dv = l_ref.shape[1] // group
    for j in range(group):
        blocks = [seq_refs[b][j] for b in range(n_seq)]
        blocks += [ctx_refs[c][0, j] for c in range(n_ctx)]
        sib = jnp.concatenate(
            [
                (sp_ref[1 + b].astype(jnp.float32) * blocks[b]).astype(jnp.bfloat16)
                for b in range(bits)
            ],
            axis=1,
        )
        for a in range(rows // TQ):
            r0 = a * TQ
            t = jnp.dot(
                q_ref[r0:r0 + TQ, j * dk:(j + 1) * dk], sib,
                preferred_element_type=jnp.float32,
            )
            w_all = m_ref[j, r0:r0 + TQ, first_level:first_level + bits] * scale
            cross = w_all[:, 0:1] * t[:, 0:dv]
            for b in range(1, bits):
                cross = cross + w_all[:, b:b + 1] * t[:, b * dv:(b + 1) * dv]
            o_ref[r0:r0 + TQ, j * dv:(j + 1) * dv] = (
                l_ref[r0:r0 + TQ, j * dv:(j + 1) * dv] + cross
            )


def cross_all(queries, scalars, seq_sibs, ctx_stacks, mix_t, local, scale, first_level, group):
    rows = queries.shape[0]
    head_count = mix_t.shape[0]
    dk = queries.shape[1] // head_count
    levels = mix_t.shape[2]
    dv = local.shape[1] // head_count
    n_seq = len(seq_sibs)
    n_ctx = len(ctx_stacks)
    bits = n_seq + n_ctx
    in_specs = [
        pl.BlockSpec((rows, dk * group), lambda g, sp: (0, g)),
        pl.BlockSpec((group, rows, levels), lambda g, sp: (g, 0, 0)),
        pl.BlockSpec((rows, dv * group), lambda g, sp: (0, g)),
    ]
    for x in seq_sibs:
        in_specs.append(pl.BlockSpec((group, dk, dv), lambda g, sp: (g, 0, 0)))
    for x in ctx_stacks:
        in_specs.append(
            pl.BlockSpec((1, group, dk, dv), lambda g, sp: (jnp.bitwise_xor(sp[0], g), 0, 0, 0))
        )
    return pl.pallas_call(
        functools.partial(cross_kernel, scale, rows, first_level, group, n_seq, n_ctx),
        grid_spec=pltpu.PrefetchScalarGridSpec(
            num_scalar_prefetch=1,
            grid=(head_count // group,),
            in_specs=in_specs,
            out_specs=pl.BlockSpec((rows, dv * group), lambda g, sp: (0, g)),
        ),
        out_shape=jax.ShapeDtypeStruct((rows, dv * head_count), jnp.float32),
        input_output_aliases={3: 0},
        cost_estimate=pl.CostEstimate(
            flops=2 * rows * dk * dv * bits * head_count,
            bytes_accessed=(2 * rows * dk + 8 * rows * dv) * head_count,
            transcendentals=0,
        ),
        compiler_params=pltpu.CompilerParams(vmem_limit_bytes=64 * 1024 * 1024),
    )(scalars, queries, mix_t, local, *seq_sibs, *ctx_stacks)


def swap(block, axis, bit, one_way=False):
    count = lax.axis_size(axis)
    route = []
    for low in range(count):
        high = low | 1 << bit
        if high != low and high < count:
            route.append((low, high))
            if not one_way:
                route.append((high, low))
    return lax.ppermute(block, axis, route)


def to_offset(block, axis, offset):
    count = lax.axis_size(axis)
    return lax.ppermute(block, axis, [(s, s ^ offset) for s in range(count)])


def shards(queries, keys, values, mixing):
    rows = queries.shape[0]
    head_count = mixing.shape[1]
    dk = queries.shape[1] // head_count
    scale = dk ** (-0.5)
    level_count = (rows // SPAN).bit_length()
    mix_t = mixing.transpose(1, 2, 0)
    masks = jnp.asarray(level_masks(TQ, level_count))

    state = own_state(keys, values, head_count)

    seq_count = lax.axis_size("seq")
    ctx_count = lax.axis_size("ctx")
    seq_bits = seq_count.bit_length() - 1
    ctx_bits = ctx_count.bit_length() - 1
    seq_place = lax.axis_index("seq")
    ctx_place = lax.axis_index("ctx")

    sibs = []
    flags = []
    running = state
    half = head_count // 2
    for bit in range(seq_bits):
        if bit == 0 and seq_count >= 4:
            mine = seq_place & 1
            needed = swap(lax.dynamic_slice_in_dim(state, (1 - mine) * half, half, 0), "seq", 0)
            rest_half = swap(lax.dynamic_slice_in_dim(state, mine * half, half, 0), "seq", 0)
            partner = jnp.concatenate(
                [jnp.where(mine == 0, needed, rest_half), jnp.where(mine == 0, rest_half, needed)],
                axis=0,
            )
        elif bit == 0 or seq_count < 4:
            partner = swap(running, "seq", bit)
        else:
            mine = seq_place & 1
            if bit == 1:
                sent = lax.dynamic_slice_in_dim(
                    lax.optimization_barrier(state), mine * half, half, 0
                ) + lax.optimization_barrier(needed)
            else:
                sent = lax.dynamic_slice_in_dim(running, mine * half, half, 0)
            got = swap(sent, "seq", bit)
            other = swap(got, "seq", 0)
            lo = jnp.where(mine == 0, got, other)
            hi = jnp.where(mine == 0, other, got)
            partner = jnp.concatenate([lo, hi], axis=0)
        sibs.append(partner)
        flags.append(seq_place >> bit & 1)
        running = running + partner

    share = head_count // seq_count
    if seq_bits == 2:
        start = seq_place * share
        inner_at = start % half
        from_got = (seq_place >> 1) == (seq_place & 1)
        upper = jnp.where(
            from_got,
            lax.dynamic_slice_in_dim(got, inner_at, share, 0),
            lax.dynamic_slice_in_dim(other, inner_at, share, 0),
        )
        quarter = (
            lax.dynamic_slice_in_dim(lax.optimization_barrier(state), start, share, 0)
            + lax.dynamic_slice_in_dim(sibs[0], start, share, 0)
        ) + upper
    else:
        quarter = lax.dynamic_slice_in_dim(running, seq_place * share, share, 0)
    ctx_sibs = []
    for bit in range(ctx_bits):
        got = swap(quarter, "ctx", bit, one_way=(bit == ctx_bits - 1))
        ctx_sibs.append(got)
        if bit != ctx_bits - 1:
            quarter = quarter + got

    ctx_stacks = []
    for bit in range(ctx_bits):
        part = lax.optimization_barrier(ctx_sibs[bit])
        parts = {0: part}
        for offset in range(1, seq_count):
            if offset & 1 and offset > 1:
                parts[offset] = to_offset(parts[offset ^ 1], "seq", 1)
            else:
                parts[offset] = to_offset(part, "seq", offset)
        ctx_stacks.append(jnp.stack([parts[o] for o in range(seq_count)]))
        flags.append(ctx_place >> bit & 1)
    scalars = jnp.stack([seq_place] + flags).astype(jnp.int32)

    per = head_count // CHUNKS
    local = None
    for c in range(CHUNKS):
        local = local_part(
            queries, keys, values, mix_t, masks, c * per, per, LOCAL_GROUP, scale, local
        )
    return cross_all(
        queries, scalars, sibs, ctx_stacks, mix_t, local, scale, level_count,
        head_count // seq_count,
    )


def solution(mesh):
    return jax.shard_map(
        shards,
        mesh=mesh,
        in_specs=(
            P(("ctx", "seq"), None),
            P(("ctx", "seq"), None),
            P(("ctx", "seq"), None),
            P(None, None, ("ctx", "seq")),
        ),
        out_specs=P(("ctx", "seq"), None),
        check_vma=False,
    )
```
